128 devices in a mesh: dom: 16 (over y, z), sub: 8 (over x, core).
Axes of the slice: x: 4, y: 4, z: 4, core: 2. Of those that a mesh axis runs over, the one named last changes fastest.
Arguments:
- history: bfloat16 [131072, 256], P(('dom', 'sub')), may hold values from -140 to 140
- tile_weight: bfloat16 [1024, 64, 128, 128], P(('dom', 'sub')), may hold values from 0 to 1.75, as said below
- tile_source: int32 [1024, 64], P(('dom', 'sub')), may hold values from 0 to 95
- tile_live: int32 [1024], P(('dom', 'sub')), may hold values from 8 to 64, as said below
- send_list: int32 [128, 16, 2], P(('dom', 'sub')), may hold values from 0 to 7
- degree: int32 [131072], P(('dom', 'sub')), may hold values from 16 to 64
- labels: int32 [131072], P(('dom', 'sub')), may hold values from 0 to 171
- neigh_weight: bfloat16 [256, 172], replicated, may hold values from -0.375 to 0.375
- self_weight: bfloat16 [256, 172], replicated, may hold values from -0.375 to 0.375
Outputs:
- grad_history: float32 [131072, 256], P(('dom', 'sub'))
- neigh_grad: float32 [256, 172], replicated
- self_grad: float32 [256, 172], replicated
The draws below stay inside these ranges and needn't reach their ends.
Inputs may be any that keep to these rules, and one draw needn't show every extreme that they name: `tile_live`: every device owns a block with all 64 tiles live. `tile_weight`: nonzero entries lie within 0.25 and 1.75.
All inputs are finite; a program needn't handle non-finite values.
Results may differ from the reference program's by a relative error of at most 0.0055.
Values may be sent and summed in bfloat16 or wider, within the bound.
No kernel may reach another device: no remote copies, remote signals or barrier semaphores. Data moves between devices by JAX's collectives and lax.ppermute only.
A program may use at most 192 MiB of HBM per device.

```python
import jax
import jax.numpy as jnp
from jax import lax

F = 256
C = 172
BLK = 128
NB_DEV = 8
TILES = 64
HALO_DEV = 32
NB_PART = 64
SLOTS = 2
SRC = 96
NODE_BLOCKS = 1024
NODES = 131072
N_DOM = 16
N_SUB = 8


def draw_history(key, part):
    values = jax.random.truncated_normal(key, -4.0, 4.0, (NODES, F), jnp.float32)
    return values.astype(jnp.bfloat16)


def draw_tile_weight(key, part):
    keys = jax.random.split(key, 2)
    shape = (NODE_BLOCKS, TILES, BLK, BLK)
    present = jax.random.randint(keys[0], shape, 0, 16) == 0
    values = jax.random.uniform(keys[1], shape, jnp.float32, 0.5, 1.5)
    return jnp.where(present, values, 0.0).astype(jnp.bfloat16)


def draw_tile_live(key, part):
    keys = jax.random.split(key, 2)
    floor_live = max(TILES // 8, 1)
    owners = NODE_BLOCKS // NB_DEV
    lowest = jax.random.randint(keys[0], (owners, 1), floor_live, TILES // 2 + 1)
    counts = jax.random.randint(keys[1], (owners, NB_DEV), lowest, TILES + 1)
    counts = counts.at[:, 0].set(TILES)
    return counts.reshape(-1).astype(jnp.int32)


def touch_ends(array, stream_key, smallest, largest):
    longest = array.shape.index(max(array.shape))
    spots = []
    for shift in (0, 1):
        where = [jax.random.randint(jax.random.fold_in(stream_key, axis), (), 0, length) for axis, length in enumerate(array.shape)]
        where[longest] = (where[longest] + shift) % array.shape[longest]
        spots.append(tuple(where))
    return array.at[spots[0]].set(smallest).at[spots[1]].set(largest)


def centred(rng, dims, spread, limit, kind=jnp.bfloat16):
    array = jax.random.normal(rng, dims, jnp.float32) * spread
    return jnp.minimum(jnp.maximum(array, -limit), limit).astype(kind)


def setup_inputs(seed: int = 0) -> dict:
    arg_keys = jax.random.split(jax.random.key(seed), 10)
    history = draw_history(jax.random.fold_in(arg_keys[9], 71), 0)
    tile_weight = draw_tile_weight(jax.random.fold_in(arg_keys[9], 71), 0)
    tile_source = touch_ends(jax.random.randint(arg_keys[2], (NODE_BLOCKS, TILES), 0, NB_DEV * N_SUB + HALO_DEV), jax.random.fold_in(arg_keys[2], 1), 0, (NB_DEV * N_SUB + HALO_DEV) - 1).astype(jnp.int32)
    tile_live = draw_tile_live(jax.random.fold_in(arg_keys[9], 71), 0)
    send_list = touch_ends(jax.random.randint(arg_keys[4], (N_DOM * N_SUB, N_DOM, SLOTS), 0, NB_DEV), jax.random.fold_in(arg_keys[4], 1), 0, NB_DEV - 1).astype(jnp.int32)
    degree = touch_ends(jax.random.randint(arg_keys[5], (NODES,), 16, 65), jax.random.fold_in(arg_keys[5], 1), 16, 64).astype(jnp.int32)
    labels = touch_ends(jax.random.randint(arg_keys[6], (NODES,), 0, C), jax.random.fold_in(arg_keys[6], 1), 0, C - 1).astype(jnp.int32)
    neigh_weight = centred(arg_keys[7], (F, C), F ** -0.5, 0.375)
    self_weight = centred(arg_keys[8], (F, C), F ** -0.5, 0.375)
    return {"history": history, "tile_weight": tile_weight, "tile_source": tile_source, "tile_live": tile_live, "send_list": send_list, "degree": degree, "labels": labels, "neigh_weight": neigh_weight, "self_weight": self_weight}


def live_mask(live_count):
    return (jnp.arange(TILES, dtype=jnp.int32)[None, :] < live_count[:, None]).astype(jnp.float32)


def halo_index(device, send_list):
    dom_index = device // N_SUB
    sub_index = device % N_SUB
    senders = jnp.arange(N_DOM, dtype=jnp.int32) * N_SUB + sub_index
    return (senders[:, None] * NB_DEV + send_list[senders, dom_index, :]).astype(jnp.int32)


def reference(history, tile_weight, tile_source, tile_live, send_list, degree, labels, neigh_weight, self_weight):
    devices_all = N_DOM * N_SUB
    blocks = history.reshape(NODE_BLOCKS, BLK, F)
    tile_block = tile_weight.reshape(devices_all, NB_DEV, TILES, BLK, BLK)
    source_dev = tile_source.reshape(devices_all, NB_DEV, TILES)
    live_dev = tile_live.reshape(devices_all, NB_DEV)
    deg_float = degree.astype(jnp.float32)
    deg_dev = deg_float.reshape(devices_all, NB_DEV, BLK)
    device_ids = jnp.arange(devices_all, dtype=jnp.int32)

    def forward(record):
        device, tiles_here, source_here, live_here, deg_here = record
        dom_index = device // N_SUB
        part_blocks = lax.dynamic_slice_in_dim(blocks, (dom_index * NB_PART).astype(jnp.int32), NB_PART, 0)
        halo_blocks = blocks[halo_index(device, send_list).reshape(-1)]
        sources = jnp.concatenate([part_blocks, halo_blocks], axis=0)
        gathered = sources[source_here].astype(jnp.float32)
        weights = tiles_here.astype(jnp.float32) * live_mask(live_here)[:, :, None, None]
        summed = jnp.einsum('btij,btjf->bif', weights, gathered, precision=lax.Precision.HIGHEST)
        return (summed / deg_here[:, :, None]).astype(jnp.bfloat16)

    aggregate = lax.map(forward, (device_ids, tile_block, source_dev, live_dev, deg_dev)).reshape(NODES, F)
    logits = jnp.dot(aggregate, neigh_weight, preferred_element_type=jnp.float32) + jnp.dot(history, self_weight, preferred_element_type=jnp.float32)
    predicted = jax.nn.softmax(logits, axis=-1)
    onehot = (labels[:, None] == jnp.arange(C, dtype=jnp.int32)[None, :]).astype(jnp.float32)
    residual = predicted - onehot
    delta = residual.astype(jnp.bfloat16)
    norm_factor = float(NODES) ** -0.5
    neigh_grad = jnp.dot(aggregate.T, delta, preferred_element_type=jnp.float32) * norm_factor
    self_grad = jnp.dot(history.T, delta, preferred_element_type=jnp.float32) * norm_factor
    scaled = (residual / deg_float[:, None]).astype(jnp.bfloat16)
    scaled_dev = scaled.reshape(devices_all, NB_DEV, BLK, C)

    def backward(record):
        tiles_here, source_here, live_here, scaled_here = record
        weights = tiles_here.astype(jnp.float32) * live_mask(live_here)[:, :, None, None]
        per_tile = jnp.einsum('btij,bic->btjc', weights, scaled_here.astype(jnp.float32), precision=lax.Precision.HIGHEST)
        by_source = jax.ops.segment_sum(per_tile.reshape(NB_DEV * TILES, BLK, C), source_here.reshape(-1), num_segments=SRC)
        return by_source[:NB_PART].astype(jnp.bfloat16), by_source[NB_PART:]

    local_parts, halo_parts = lax.map(backward, (tile_block, source_dev, live_dev, scaled_dev))
    local_grad = local_parts.astype(jnp.float32).reshape(N_DOM, N_SUB, NB_PART, BLK, C).sum(axis=1).reshape(NODE_BLOCKS, BLK, C)
    targets = lax.map(lambda device: halo_index(device, send_list), device_ids).reshape(-1)
    boundary_grad = jax.ops.segment_sum(halo_parts.reshape(devices_all * HALO_DEV, BLK, C), targets, num_segments=NODE_BLOCKS)
    backward_sum = (local_grad + boundary_grad).reshape(NODES, C)
    grad_history = jnp.dot(backward_sum, neigh_weight.astype(jnp.float32).T, precision=lax.Precision.HIGHEST) + jnp.dot(delta, self_weight.T, preferred_element_type=jnp.float32)
    return (grad_history, neigh_grad, self_grad)
```

```python
import functools

import jax
import jax.numpy as jnp
from jax import lax
from jax.experimental import pallas as pl
from jax.experimental.pallas import tpu as pltpu
from jax.sharding import PartitionSpec as P

LANES = 128


def _fused_kernel(
    src_ref,
    live_ref,
    w_ref,
    sources_ref,
    hist_ref,
    deg_ref,
    lab_ref,
    nw_ref,
    sw_ref,
    swt_ref,
    term_ref,
    grads_ref,
    selfterm_ref,
    *,
    classes,
):
    b = pl.program_id(0)
    rows = w_ref.shape[2]
    width = sources_ref.shape[2]
    padded = nw_ref.shape[1]

    @pl.when(b == 0)
    def _():
        term_ref[...] = jnp.zeros_like(term_ref)
        grads_ref[...] = jnp.zeros_like(grads_ref)

    live = live_ref[b]

    def forward(t, acc):
        s = src_ref[b, t]
        return acc + jnp.dot(w_ref[0, t], sources_ref[s], preferred_element_type=jnp.float32)

    acc = lax.fori_loop(0, live, forward, jnp.zeros((rows, width), jnp.float32))
    deg = deg_ref[0]
    aggregate = (acc / deg).astype(jnp.bfloat16)
    own = hist_ref[0]
    logits = jnp.dot(aggregate, nw_ref[...], preferred_element_type=jnp.float32) + jnp.dot(
        own, sw_ref[...], preferred_element_type=jnp.float32
    )
    col = lax.broadcasted_iota(jnp.int32, (rows, padded), 1)
    logits = jnp.where(col < classes, logits, -1e30)
    top = jnp.max(logits, axis=-1, keepdims=True)
    expd = jnp.exp(logits - top)
    predicted = expd / jnp.sum(expd, axis=-1, keepdims=True)
    onehot = (col == lab_ref[0]).astype(jnp.float32)
    residual = predicted - onehot
    delta = residual.astype(jnp.bfloat16)
    tn = (((0,), (0,)), ((), ()))
    grads_ref[0] += lax.dot_general(aggregate, delta, tn, preferred_element_type=jnp.float32)
    grads_ref[1] += lax.dot_general(own, delta, tn, preferred_element_type=jnp.float32)
    selfterm_ref[0] = jnp.dot(delta, swt_ref[...], preferred_element_type=jnp.float32)
    scaled = (residual / deg).astype(jnp.bfloat16)

    def backward(t, carry):
        s = src_ref[b, t]
        term_ref[s] += lax.dot_general(w_ref[0, t], scaled, tn, preferred_element_type=jnp.float32)
        return carry

    lax.fori_loop(0, live, backward, 0)


def _fused(tile_source, tile_live, tile_weight, sources, own_blocks, deg, lab, nw, sw, swt, classes):
    block_count, tile_slots, rows, _ = tile_weight.shape
    source_total, _, width = sources.shape
    padded = nw.shape[1]
    vmem = pltpu.MemorySpace.VMEM if hasattr(pltpu, "MemorySpace") else pltpu.VMEM
    grid_spec = pltpu.PrefetchScalarGridSpec(
        num_scalar_prefetch=2,
        grid=(block_count,),
        in_specs=[
            pl.BlockSpec((1, tile_slots, rows, rows), lambda b, *_: (b, 0, 0, 0)),
            pl.BlockSpec(memory_space=vmem),
            pl.BlockSpec((1, rows, width), lambda b, *_: (b, 0, 0)),
            pl.BlockSpec((1, rows, 1), lambda b, *_: (b, 0, 0)),
            pl.BlockSpec((1, rows, 1), lambda b, *_: (b, 0, 0)),
            pl.BlockSpec(memory_space=vmem),
            pl.BlockSpec(memory_space=vmem),
            pl.BlockSpec(memory_space=vmem),
        ],
        out_specs=[
            pl.BlockSpec(memory_space=vmem),
            pl.BlockSpec(memory_space=vmem),
            pl.BlockSpec((1, rows, width), lambda b, *_: (b, 0, 0)),
        ],
    )
    return pl.pallas_call(
        functools.partial(_fused_kernel, classes=classes),
        grid_spec=grid_spec,
        out_shape=[
            jax.ShapeDtypeStruct((source_total, rows, padded), jnp.float32),
            jax.ShapeDtypeStruct((2, width, padded), jnp.float32),
            jax.ShapeDtypeStruct((block_count, rows, width), jnp.float32),
        ],
        compiler_params=pltpu.CompilerParams(
            dimension_semantics=("arbitrary",), vmem_limit_bytes=56 * 1024 * 1024
        ),
    )(tile_source, tile_live, tile_weight, sources, own_blocks, deg, lab, nw, sw, swt)


def per_device(
    history,
    tile_weight,
    tile_source,
    tile_live,
    send_list,
    degree,
    labels,
    neigh_weight,
    self_weight,
):
    block_count = tile_weight.shape[0]
    block_rows = tile_weight.shape[2]
    width = history.shape[1]
    classes = neigh_weight.shape[1]
    dom_count = lax.axis_size("dom")
    sub_count = lax.axis_size("sub")
    devices_all = dom_count * sub_count
    nodes_all = history.shape[0] * devices_all
    padded = -(-classes // LANES) * LANES
    own_blocks = history.reshape(block_count, block_rows, width)
    partition = lax.all_gather(own_blocks, "sub", axis=0, tiled=True)
    part_blocks = partition.shape[0]
    own_ids = jnp.arange(block_count, dtype=jnp.int32)
    send_table = send_list[0][:, :, None] == own_ids[None, None, :]
    outgoing = jnp.einsum(
        "pks,sif->pkif",
        send_table.astype(jnp.bfloat16),
        own_blocks,
        preferred_element_type=jnp.float32,
    ).astype(jnp.bfloat16)
    boundary = lax.all_to_all(outgoing, "dom", split_axis=0, concat_axis=0, tiled=True)
    slot_count = boundary.shape[1]
    sources = jnp.concatenate(
        [partition, boundary.reshape(dom_count * slot_count, block_rows, width)], axis=0
    )
    degrees = degree.astype(jnp.float32).reshape(block_count, block_rows, 1)
    lab = labels.reshape(block_count, block_rows, 1)
    pad_cols = ((0, 0), (0, padded - classes))
    nw = jnp.pad(neigh_weight, pad_cols)
    sw = jnp.pad(self_weight, pad_cols)
    swt = jnp.pad(self_weight.T, ((0, padded - classes), (0, 0)))
    term, grads, selfterm = _fused(
        tile_source, tile_live, tile_weight, sources, own_blocks, degrees, lab, nw, sw, swt, classes
    )

    flat = grads[:, :, :classes].reshape(devices_all, -1)
    mine = lax.all_to_all(flat, ("dom", "sub"), 0, 0, tiled=True).sum(axis=0, keepdims=True)
    spread = jnp.broadcast_to(mine, (devices_all, mine.shape[1]))
    totals = lax.all_to_all(spread, ("dom", "sub"), 0, 0, tiled=True).reshape(2, width, classes)
    norm_factor = float(nodes_all) ** (-0.5)

    local = term[:part_blocks, :, :classes].astype(jnp.bfloat16)
    local = local.reshape(sub_count, block_count, block_rows, classes)
    local_grad = (
        lax.all_to_all(local, "sub", 0, 0, tiled=True).astype(jnp.float32).sum(axis=0)
    )
    halo = term[part_blocks:, :, :classes].astype(jnp.bfloat16)
    halo = halo.reshape(dom_count, slot_count, block_rows, classes)
    arrived = lax.all_to_all(halo, "dom", 0, 0, tiled=True).astype(jnp.float32)
    return_table = send_table.astype(jnp.float32)
    incoming = jnp.einsum("pks,pkic->sic", return_table, arrived, precision=lax.Precision.HIGHEST)
    backward_sum = (local_grad + incoming).reshape(-1, classes)
    neigh_float = neigh_weight.astype(jnp.float32)
    grad_history = jnp.dot(
        backward_sum, neigh_float.T, precision=lax.Precision.HIGHEST
    ) + selfterm.reshape(-1, width)
    return (grad_history, totals[0] * norm_factor, totals[1] * norm_factor)


def solution(mesh):
    placed = (
        P(("dom", "sub"), None),
        P(("dom", "sub"), None, None, None),
        P(("dom", "sub"), None),
        P(("dom", "sub")),
        P(("dom", "sub"), None, None),
        P(("dom", "sub")),
        P(("dom", "sub")),
        P(),
        P(),
    )
    return jax.shard_map(
        per_device,
        mesh=mesh,
        in_specs=placed,
        out_specs=(P(("dom", "sub"), None), P(), P()),
        check_vma=False,
    )
```

```python
import functools

import jax
import jax.numpy as jnp
from jax import lax
from jax.experimental import pallas as pl
from jax.experimental.pallas import tpu as pltpu
from jax.sharding import PartitionSpec as P

LANES = 128
GROUP = 8


def _fused_kernel(
    src_ref,
    live_ref,
    w_ref,
    sources_ref,
    hist_ref,
    deg_ref,
    lab_ref,
    nw_ref,
    sw_ref,
    swt_ref,
    term_ref,
    grads_ref,
    selfterm_ref,
    *,
    classes,
):
    b = pl.program_id(0)
    rows = w_ref.shape[2]
    width = sources_ref.shape[2]
    padded = nw_ref.shape[1]

    @pl.when(b == 0)
    def _():
        term_ref[...] = jnp.zeros_like(term_ref)
        grads_ref[...] = jnp.zeros_like(grads_ref)

    live = live_ref[b]
    groups = (live + GROUP - 1) // GROUP

    def tile(t):
        return jnp.where(t < live, w_ref[0, t], jnp.zeros_like(w_ref[0, t]))

    def forward(g, acc):
        for k in range(GROUP):
            t = g * GROUP + k
            acc = acc + jnp.dot(tile(t), sources_ref[src_ref[b, t]], preferred_element_type=jnp.float32)
        return acc

    acc = lax.fori_loop(0, groups, forward, jnp.zeros((rows, width), jnp.float32))
    deg = deg_ref[0]
    aggregate = (acc / deg).astype(jnp.bfloat16)
    own = hist_ref[0]
    logits = jnp.dot(aggregate, nw_ref[...], preferred_element_type=jnp.float32) + jnp.dot(
        own, sw_ref[...], preferred_element_type=jnp.float32
    )
    col = lax.broadcasted_iota(jnp.int32, (rows, padded), 1)
    logits = jnp.where(col < classes, logits, -1e30)
    top = jnp.max(logits, axis=-1, keepdims=True)
    expd = jnp.exp(logits - top)
    predicted = expd / jnp.sum(expd, axis=-1, keepdims=True)
    onehot = (col == lab_ref[0]).astype(jnp.float32)
    residual = predicted - onehot
    delta = residual.astype(jnp.bfloat16)
    tn = (((0,), (0,)), ((), ()))
    grads_ref[0] += lax.dot_general(aggregate, delta, tn, preferred_element_type=jnp.float32)
    grads_ref[1] += lax.dot_general(own, delta, tn, preferred_element_type=jnp.float32)
    selfterm_ref[0] = jnp.dot(delta, swt_ref[...], preferred_element_type=jnp.float32)
    scaled_t = (residual / deg).astype(jnp.bfloat16).T

    def backward(g, carry):
        for k in range(GROUP):
            t = g * GROUP + k
            s = src_ref[b, t]
            term_ref[s] += jnp.dot(scaled_t, tile(t), preferred_element_type=jnp.float32)
        return carry

    lax.fori_loop(0, groups, backward, 0)


def _fused(tile_source, tile_live, tile_weight, sources, own_blocks, deg, lab, nw, sw, swt, classes):
    block_count, tile_slots, rows, _ = tile_weight.shape
    source_total, _, width = sources.shape
    padded = nw.shape[1]
    vmem = pltpu.MemorySpace.VMEM if hasattr(pltpu, "MemorySpace") else pltpu.VMEM
    grid_spec = pltpu.PrefetchScalarGridSpec(
        num_scalar_prefetch=2,
        grid=(block_count,),
        in_specs=[
            pl.BlockSpec((1, tile_slots, rows, rows), lambda b, *_: (b, 0, 0, 0)),
            pl.BlockSpec(memory_space=vmem),
            pl.BlockSpec((1, rows, width), lambda b, *_: (b, 0, 0)),
            pl.BlockSpec((1, rows, 1), lambda b, *_: (b, 0, 0)),
            pl.BlockSpec((1, rows, 1), lambda b, *_: (b, 0, 0)),
            pl.BlockSpec(memory_space=vmem),
            pl.BlockSpec(memory_space=vmem),
            pl.BlockSpec(memory_space=vmem),
        ],
        out_specs=[
            pl.BlockSpec(memory_space=vmem),
            pl.BlockSpec(memory_space=vmem),
            pl.BlockSpec((1, rows, width), lambda b, *_: (b, 0, 0)),
        ],
    )
    return pl.pallas_call(
        functools.partial(_fused_kernel, classes=classes),
        grid_spec=grid_spec,
        out_shape=[
            jax.ShapeDtypeStruct((source_total, padded, rows), jnp.float32),
            jax.ShapeDtypeStruct((2, width, padded), jnp.float32),
            jax.ShapeDtypeStruct((block_count, rows, width), jnp.float32),
        ],
        compiler_params=pltpu.CompilerParams(
            dimension_semantics=("arbitrary",), vmem_limit_bytes=56 * 1024 * 1024
        ),
    )(tile_source, tile_live, tile_weight, sources, own_blocks, deg, lab, nw, sw, swt)


def per_device(
    history,
    tile_weight,
    tile_source,
    tile_live,
    send_list,
    degree,
    labels,
    neigh_weight,
    self_weight,
):
    block_count = tile_weight.shape[0]
    block_rows = tile_weight.shape[2]
    width = history.shape[1]
    classes = neigh_weight.shape[1]
    dom_count = lax.axis_size("dom")
    sub_count = lax.axis_size("sub")
    devices_all = dom_count * sub_count
    nodes_all = history.shape[0] * devices_all
    padded = -(-classes // LANES) * LANES
    own_blocks = history.reshape(block_count, block_rows, width)
    partition = lax.all_gather(own_blocks, "sub", axis=0, tiled=True)
    part_blocks = partition.shape[0]
    own_ids = jnp.arange(block_count, dtype=jnp.int32)
    send_table = send_list[0][:, :, None] == own_ids[None, None, :]
    outgoing = jnp.einsum(
        "pks,sif->pkif",
        send_table.astype(jnp.bfloat16),
        own_blocks,
        preferred_element_type=jnp.float32,
    ).astype(jnp.bfloat16)
    boundary = lax.all_to_all(outgoing, "dom", split_axis=0, concat_axis=0, tiled=True)
    slot_count = boundary.shape[1]
    sources = jnp.concatenate(
        [partition, boundary.reshape(dom_count * slot_count, block_rows, width)], axis=0
    )
    degrees = degree.astype(jnp.float32).reshape(block_count, block_rows, 1)
    lab = labels.reshape(block_count, block_rows, 1)
    pad_cols = ((0, 0), (0, padded - classes))
    nw = jnp.pad(neigh_weight, pad_cols)
    sw = jnp.pad(self_weight, pad_cols)
    swt = jnp.pad(self_weight.T, ((0, padded - classes), (0, 0)))
    term, grads, selfterm = _fused(
        tile_source, tile_live, tile_weight, sources, own_blocks, degrees, lab, nw, sw, swt, classes
    )

    flat = grads[:, :, :classes].reshape(devices_all, -1)
    mine = lax.all_to_all(flat, ("dom", "sub"), 0, 0, tiled=True).sum(axis=0, keepdims=True)
    spread = jnp.broadcast_to(mine, (devices_all, mine.shape[1]))
    totals = lax.all_to_all(spread, ("dom", "sub"), 0, 0, tiled=True).reshape(2, width, classes)
    norm_factor = float(nodes_all) ** (-0.5)

    local = term[:part_blocks, :classes].astype(jnp.bfloat16)
    local = local.reshape(sub_count, block_count, classes, block_rows)
    local_grad = (
        lax.all_to_all(local, "sub", 0, 0, tiled=True).astype(jnp.float32).sum(axis=0)
    )
    halo = term[part_blocks:, :classes].astype(jnp.bfloat16)
    halo = halo.reshape(dom_count, slot_count, classes, block_rows)
    arrived = lax.all_to_all(halo, "dom", 0, 0, tiled=True).astype(jnp.float32)
    return_table = send_table.astype(jnp.float32)
    incoming = jnp.einsum("pks,pkci->sci", return_table, arrived, precision=lax.Precision.HIGHEST)
    backward_sum = local_grad + incoming
    neigh_float = neigh_weight.astype(jnp.float32)
    grad_history = jnp.einsum(
        "sci,fc->sif", backward_sum, neigh_float, precision=lax.Precision.HIGHEST
    ).reshape(-1, width) + selfterm.reshape(-1, width)
    return (grad_history, totals[0] * norm_factor, totals[1] * norm_factor)


def solution(mesh):
    placed = (
        P(("dom", "sub"), None),
        P(("dom", "sub"), None, None, None),
        P(("dom", "sub"), None),
        P(("dom", "sub")),
        P(("dom", "sub"), None, None),
        P(("dom", "sub")),
        P(("dom", "sub")),
        P(),
        P(),
    )
    return jax.shard_map(
        per_device,
        mesh=mesh,
        in_specs=placed,
        out_specs=(P(("dom", "sub"), None), P(), P()),
        check_vma=False,
    )
```

```python
import functools

import jax
import jax.numpy as jnp
from jax import lax
from jax.experimental import pallas as pl
from jax.experimental.pallas import tpu as pltpu
from jax.sharding import PartitionSpec as P

LANES = 128
GROUP = 8


def _fused_kernel(
    src_ref,
    live_ref,
    w_ref,
    sources_ref,
    hist_ref,
    deg_ref,
    lab_ref,
    nw_ref,
    sw_ref,
    swt_ref,
    term_ref,
    grads_ref,
    selfterm_ref,
    *,
    classes,
):
    b = pl.program_id(0)
    rows = w_ref.shape[2]
    width = sources_ref.shape[2]
    padded = nw_ref.shape[1]

    @pl.when(b == 0)
    def _():
        term_ref[...] = jnp.zeros_like(term_ref)
        grads_ref[...] = jnp.zeros_like(grads_ref)

    live = live_ref[b]
    groups = (live + GROUP - 1) // GROUP

    def tile(t):
        return jnp.where(t < live, w_ref[0, t], jnp.zeros_like(w_ref[0, t]))

    def forward(g, acc):
        for k in range(GROUP):
            t = g * GROUP + k
            acc = acc + jnp.dot(tile(t), sources_ref[src_ref[b, t]], preferred_element_type=jnp.float32)
        return acc

    acc = lax.fori_loop(0, groups, forward, jnp.zeros((rows, width), jnp.float32))
    deg = deg_ref[0]
    aggregate = (acc / deg).astype(jnp.bfloat16)
    own = hist_ref[0]
    logits = jnp.dot(aggregate, nw_ref[...], preferred_element_type=jnp.float32) + jnp.dot(
        own, sw_ref[...], preferred_element_type=jnp.float32
    )
    col = lax.broadcasted_iota(jnp.int32, (rows, padded), 1)
    logits = jnp.where(col < classes, logits, -1e30)
    top = jnp.max(logits, axis=-1, keepdims=True)
    expd = jnp.exp(logits - top)
    predicted = expd / jnp.sum(expd, axis=-1, keepdims=True)
    onehot = (col == lab_ref[0]).astype(jnp.float32)
    residual = predicted - onehot
    delta = residual.astype(jnp.bfloat16)
    tn = (((0,), (0,)), ((), ()))
    grads_ref[0] += lax.dot_general(aggregate, delta, tn, preferred_element_type=jnp.float32)
    grads_ref[1] += lax.dot_general(own, delta, tn, preferred_element_type=jnp.float32)
    selfterm_ref[0] = jnp.dot(delta, swt_ref[...], preferred_element_type=jnp.float32)
    scaled_t = (residual / deg).astype(jnp.bfloat16).T

    def backward(g, carry):
        for k in range(GROUP):
            t = g * GROUP + k
            s = src_ref[b, t]
            term_ref[s] += jnp.dot(scaled_t, tile(t), preferred_element_type=jnp.float32)
        return carry

    lax.fori_loop(0, groups, backward, 0)


def _fused(tile_source, tile_live, tile_weight, sources, own_blocks, deg, lab, nw, sw, swt, classes):
    block_count, tile_slots, rows, _ = tile_weight.shape
    source_total, _, width = sources.shape
    padded = nw.shape[1]
    vmem = pltpu.MemorySpace.VMEM if hasattr(pltpu, "MemorySpace") else pltpu.VMEM
    grid_spec = pltpu.PrefetchScalarGridSpec(
        num_scalar_prefetch=2,
        grid=(block_count,),
        in_specs=[
            pl.BlockSpec((1, tile_slots, rows, rows), lambda b, *_: (b, 0, 0, 0)),
            pl.BlockSpec(memory_space=vmem),
            pl.BlockSpec((1, rows, width), lambda b, *_: (b, 0, 0)),
            pl.BlockSpec((1, rows, 1), lambda b, *_: (b, 0, 0)),
            pl.BlockSpec((1, rows, 1), lambda b, *_: (b, 0, 0)),
            pl.BlockSpec(memory_space=vmem),
            pl.BlockSpec(memory_space=vmem),
            pl.BlockSpec(memory_space=vmem),
        ],
        out_specs=[
            pl.BlockSpec(memory_space=vmem),
            pl.BlockSpec(memory_space=vmem),
            pl.BlockSpec((1, rows, width), lambda b, *_: (b, 0, 0)),
        ],
    )
    return pl.pallas_call(
        functools.partial(_fused_kernel, classes=classes),
        grid_spec=grid_spec,
        out_shape=[
            jax.ShapeDtypeStruct((source_total, padded, rows), jnp.float32),
            jax.ShapeDtypeStruct((2, width, padded), jnp.float32),
            jax.ShapeDtypeStruct((block_count, rows, width), jnp.float32),
        ],
        compiler_params=pltpu.CompilerParams(
            dimension_semantics=("arbitrary",), vmem_limit_bytes=56 * 1024 * 1024
        ),
    )(tile_source, tile_live, tile_weight, sources, own_blocks, deg, lab, nw, sw, swt)


def per_device(
    history,
    tile_weight,
    tile_source,
    tile_live,
    send_list,
    degree,
    labels,
    neigh_weight,
    self_weight,
):
    block_count = tile_weight.shape[0]
    block_rows = tile_weight.shape[2]
    width = history.shape[1]
    classes = neigh_weight.shape[1]
    dom_count = lax.axis_size("dom")
    sub_count = lax.axis_size("sub")
    devices_all = dom_count * sub_count
    nodes_all = history.shape[0] * devices_all
    padded = -(-classes // LANES) * LANES
    own_blocks = history.reshape(block_count, block_rows, width)
    partition = lax.all_gather(own_blocks, "sub", axis=0, tiled=True)
    part_blocks = partition.shape[0]
    own_ids = jnp.arange(block_count, dtype=jnp.int32)
    send_table = send_list[0][:, :, None] == own_ids[None, None, :]
    outgoing = jnp.einsum(
        "pks,sif->pkif",
        send_table.astype(jnp.bfloat16),
        own_blocks,
        preferred_element_type=jnp.float32,
    ).astype(jnp.bfloat16)
    boundary = lax.all_to_all(outgoing, "dom", split_axis=0, concat_axis=0, tiled=True)
    slot_count = boundary.shape[1]
    sources = jnp.concatenate(
        [partition, boundary.reshape(dom_count * slot_count, block_rows, width)], axis=0
    )
    degrees = degree.astype(jnp.float32).reshape(block_count, block_rows, 1)
    lab = labels.reshape(block_count, block_rows, 1)
    pad_cols = ((0, 0), (0, padded - classes))
    nw = jnp.pad(neigh_weight, pad_cols)
    sw = jnp.pad(self_weight, pad_cols)
    swt = jnp.pad(self_weight.T, ((0, padded - classes), (0, 0)))
    term, grads, selfterm = _fused(
        tile_source, tile_live, tile_weight, sources, own_blocks, degrees, lab, nw, sw, swt, classes
    )

    flat = grads[:, :, :classes].reshape(sub_count, -1)
    mine = lax.psum_scatter(flat, "sub", scatter_dimension=0, tiled=True)
    mine = lax.psum(mine, "dom")
    totals = lax.all_gather(mine, "sub", axis=0, tiled=True).reshape(2, width, classes)
    norm_factor = float(nodes_all) ** (-0.5)

    local = term[:part_blocks, :classes].astype(jnp.bfloat16)
    local = local.reshape(sub_count, block_count, classes, block_rows)
    local_grad = (
        lax.all_to_all(local, "sub", 0, 0, tiled=True).astype(jnp.float32).sum(axis=0)
    )
    halo = term[part_blocks:, :classes].astype(jnp.bfloat16)
    halo = halo.reshape(dom_count, slot_count, classes, block_rows)
    arrived = lax.all_to_all(halo, "dom", 0, 0, tiled=True).astype(jnp.float32)
    return_table = send_table.astype(jnp.float32)
    incoming = jnp.einsum("pks,pkci->sci", return_table, arrived, precision=lax.Precision.HIGHEST)
    backward_sum = local_grad + incoming
    neigh_float = neigh_weight.astype(jnp.float32)
    grad_history = jnp.einsum(
        "sci,fc->sif", backward_sum, neigh_float, precision=lax.Precision.HIGHEST
    ).reshape(-1, width) + selfterm.reshape(-1, width)
    return (grad_history, totals[0] * norm_factor, totals[1] * norm_factor)


def solution(mesh):
    placed = (
        P(("dom", "sub"), None),
        P(("dom", "sub"), None, None, None),
        P(("dom", "sub"), None),
        P(("dom", "sub")),
        P(("dom", "sub"), None, None),
        P(("dom", "sub")),
        P(("dom", "sub")),
        P(),
        P(),
    )
    return jax.shard_map(
        per_device,
        mesh=mesh,
        in_specs=placed,
        out_specs=(P(("dom", "sub"), None), P(), P()),
        check_vma=False,
    )
```

```python
import functools

import jax
import jax.numpy as jnp
from jax import lax
from jax.experimental import pallas as pl
from jax.experimental.pallas import tpu as pltpu
from jax.sharding import PartitionSpec as P

LANES = 128
GROUP = 8


def _fused_kernel(
    src_ref,
    live_ref,
    w_ref,
    sources_ref,
    hist_ref,
    deg_ref,
    lab_ref,
    nw_ref,
    sw_ref,
    swt_ref,
    out_ref,
    grads_ref,
    selfterm_ref,
    term_ref,
    *,
    classes,
):
    b = pl.program_id(0)
    rows = w_ref.shape[2]
    width = sources_ref.shape[2]
    padded = nw_ref.shape[1]

    @pl.when(b == 0)
    def _():
        term_ref[...] = jnp.zeros_like(term_ref)
        grads_ref[...] = jnp.zeros_like(grads_ref)

    live = live_ref[b]
    groups = (live + GROUP - 1) // GROUP

    def tile(t):
        return jnp.where(t < live, w_ref[0, t], jnp.zeros_like(w_ref[0, t]))

    def forward(g, acc):
        ts = [g * GROUP + k for k in range(GROUP)]
        wcat = jnp.concatenate([tile(t) for t in ts], axis=1)
        scat = jnp.concatenate([sources_ref[src_ref[b, t]] for t in ts], axis=0)
        return acc + jnp.dot(wcat, scat, preferred_element_type=jnp.float32)

    acc = lax.fori_loop(0, groups, forward, jnp.zeros((rows, width), jnp.float32))
    deg = deg_ref[0]
    aggregate = (acc / deg).astype(jnp.bfloat16)
    own = hist_ref[0]
    logits = jnp.dot(aggregate, nw_ref[...], preferred_element_type=jnp.float32) + jnp.dot(
        own, sw_ref[...], preferred_element_type=jnp.float32
    )
    col = lax.broadcasted_iota(jnp.int32, (rows, padded), 1)
    logits = jnp.where(col < classes, logits, -1e30)
    top = jnp.max(logits, axis=-1, keepdims=True)
    expd = jnp.exp(logits - top)
    predicted = expd / jnp.sum(expd, axis=-1, keepdims=True)
    onehot = (col == lab_ref[0]).astype(jnp.float32)
    residual = predicted - onehot
    delta = residual.astype(jnp.bfloat16)
    tn = (((0,), (0,)), ((), ()))
    grads_ref[0] += lax.dot_general(aggregate, delta, tn, preferred_element_type=jnp.float32)
    grads_ref[1] += lax.dot_general(own, delta, tn, preferred_element_type=jnp.float32)
    selfterm_ref[0] = jnp.dot(delta, swt_ref[...], preferred_element_type=jnp.float32)
    scaled_t = (residual / deg).astype(jnp.bfloat16).T

    def backward(g, carry):
        for k in range(GROUP):
            t = g * GROUP + k
            s = src_ref[b, t]
            term_ref[s] += jnp.dot(scaled_t, tile(t), preferred_element_type=jnp.float32)
        return carry

    lax.fori_loop(0, groups, backward, 0)

    @pl.when(b == pl.num_programs(0) - 1)
    def _():
        out_ref[...] = term_ref[:, : out_ref.shape[1], :].astype(out_ref.dtype)


def _fused(tile_source, tile_live, tile_weight, sources, own_blocks, deg, lab, nw, sw, swt, classes):
    block_count, tile_slots, rows, _ = tile_weight.shape
    source_total, _, width = sources.shape
    padded = nw.shape[1]
    kept = -(-classes // 16) * 16
    grid_spec = pltpu.PrefetchScalarGridSpec(
        num_scalar_prefetch=2,
        grid=(block_count,),
        in_specs=[
            pl.BlockSpec((1, tile_slots, rows, rows), lambda b, *_: (b, 0, 0, 0)),
            pl.BlockSpec((source_total, rows, width), lambda b, *_: (0, 0, 0)),
            pl.BlockSpec((1, rows, width), lambda b, *_: (b, 0, 0)),
            pl.BlockSpec((1, rows, 1), lambda b, *_: (b, 0, 0)),
            pl.BlockSpec((1, rows, 1), lambda b, *_: (b, 0, 0)),
            pl.BlockSpec((width, padded), lambda b, *_: (0, 0)),
            pl.BlockSpec((width, padded), lambda b, *_: (0, 0)),
            pl.BlockSpec((padded, width), lambda b, *_: (0, 0)),
        ],
        out_specs=[
            pl.BlockSpec((source_total, kept, rows), lambda b, *_: (0, 0, 0)),
            pl.BlockSpec((2, width, padded), lambda b, *_: (0, 0, 0)),
            pl.BlockSpec((1, rows, width), lambda b, *_: (b, 0, 0)),
        ],
        scratch_shapes=[pltpu.VMEM((source_total, padded, rows), jnp.float32)],
    )
    return pl.pallas_call(
        functools.partial(_fused_kernel, classes=classes),
        grid_spec=grid_spec,
        out_shape=[
            jax.ShapeDtypeStruct((source_total, kept, rows), jnp.bfloat16),
            jax.ShapeDtypeStruct((2, width, padded), jnp.float32),
            jax.ShapeDtypeStruct((block_count, rows, width), jnp.float32),
        ],
        compiler_params=pltpu.CompilerParams(
            dimension_semantics=("arbitrary",), vmem_limit_bytes=60 * 1024 * 1024
        ),
    )(tile_source, tile_live, tile_weight, sources, own_blocks, deg, lab, nw, sw, swt)


def per_device(
    history,
    tile_weight,
    tile_source,
    tile_live,
    send_list,
    degree,
    labels,
    neigh_weight,
    self_weight,
):
    block_count = tile_weight.shape[0]
    block_rows = tile_weight.shape[2]
    width = history.shape[1]
    classes = neigh_weight.shape[1]
    dom_count = lax.axis_size("dom")
    sub_count = lax.axis_size("sub")
    devices_all = dom_count * sub_count
    nodes_all = history.shape[0] * devices_all
    padded = -(-classes // LANES) * LANES
    own_blocks = history.reshape(block_count, block_rows, width)
    partition = lax.all_gather(own_blocks, "sub", axis=0, tiled=True)
    part_blocks = partition.shape[0]
    own_ids = jnp.arange(block_count, dtype=jnp.int32)
    send_table = send_list[0][:, :, None] == own_ids[None, None, :]
    outgoing = jnp.einsum(
        "pks,sif->pkif",
        send_table.astype(jnp.bfloat16),
        own_blocks,
        preferred_element_type=jnp.float32,
    ).astype(jnp.bfloat16)
    boundary = lax.all_to_all(outgoing, "dom", split_axis=0, concat_axis=0, tiled=True)
    slot_count = boundary.shape[1]
    sources = jnp.concatenate(
        [partition, boundary.reshape(dom_count * slot_count, block_rows, width)], axis=0
    )
    degrees = degree.astype(jnp.float32).reshape(block_count, block_rows, 1)
    lab = labels.reshape(block_count, block_rows, 1)
    pad_cols = ((0, 0), (0, padded - classes))
    nw = jnp.pad(neigh_weight, pad_cols)
    sw = jnp.pad(self_weight, pad_cols)
    swt = jnp.pad(self_weight.T, ((0, padded - classes), (0, 0)))
    term, grads, selfterm = _fused(
        tile_source, tile_live, tile_weight, sources, own_blocks, degrees, lab, nw, sw, swt, classes
    )

    flat = grads[:, :, :classes].reshape(devices_all, -1)
    mine = lax.all_to_all(flat, ("dom", "sub"), 0, 0, tiled=True).sum(axis=0, keepdims=True)
    spread = jnp.broadcast_to(mine, (devices_all, mine.shape[1]))
    totals = lax.all_to_all(spread, ("dom", "sub"), 0, 0, tiled=True).reshape(2, width, classes)
    norm_factor = float(nodes_all) ** (-0.5)

    local = term[:part_blocks, :classes]
    local = local.reshape(sub_count, block_count, classes, block_rows)
    local_grad = (
        lax.all_to_all(local, "sub", 0, 0, tiled=True).astype(jnp.float32).sum(axis=0)
    )
    halo = term[part_blocks:, :classes]
    halo = halo.reshape(dom_count, slot_count, classes, block_rows)
    arrived = lax.all_to_all(halo, "dom", 0, 0, tiled=True).astype(jnp.float32)
    return_table = send_table.astype(jnp.float32)
    incoming = jnp.einsum("pks,pkci->sci", return_table, arrived, precision=lax.Precision.HIGHEST)
    backward_sum = local_grad + incoming
    neigh_float = neigh_weight.astype(jnp.float32)
    grad_history = jnp.einsum(
        "sci,fc->sif", backward_sum, neigh_float, precision=lax.Precision.HIGHEST
    ).reshape(-1, width) + selfterm.reshape(-1, width)
    return (grad_history, totals[0] * norm_factor, totals[1] * norm_factor)


def solution(mesh):
    placed = (
        P(("dom", "sub"), None),
        P(("dom", "sub"), None, None, None),
        P(("dom", "sub"), None),
        P(("dom", "sub")),
        P(("dom", "sub"), None, None),
        P(("dom", "sub")),
        P(("dom", "sub")),
        P(),
        P(),
    )
    return jax.shard_map(
        per_device,
        mesh=mesh,
        in_specs=placed,
        out_specs=(P(("dom", "sub"), None), P(), P()),
        check_vma=False,
    )
```

```python
import functools

import jax
import jax.numpy as jnp
from jax import lax
from jax.experimental import pallas as pl
from jax.experimental.pallas import tpu as pltpu
from jax.sharding import PartitionSpec as P

LANES = 128
GROUP = 8


def _fused_kernel(
    src_ref,
    live_ref,
    w_ref,
    sources_ref,
    hist_ref,
    deg_ref,
    lab_ref,
    nw_ref,
    sw_ref,
    swt_ref,
    out_ref,
    grads_ref,
    selfterm_ref,
    term_ref,
    *,
    classes,
):
    b = pl.program_id(0)
    rows = w_ref.shape[2]
    width = sources_ref.shape[2]
    padded = nw_ref.shape[1]

    @pl.when(b == 0)
    def _():
        term_ref[...] = jnp.zeros_like(term_ref)
        grads_ref[...] = jnp.zeros_like(grads_ref)

    live = live_ref[b]
    groups = (live + GROUP - 1) // GROUP

    def tile(t):
        return jnp.where(t < live, w_ref[0, t], jnp.zeros_like(w_ref[0, t]))

    def forward(g, acc):
        ts = [g * GROUP + k for k in range(GROUP)]
        wcat = jnp.concatenate([tile(t) for t in ts], axis=1)
        scat = jnp.concatenate([sources_ref[src_ref[b, t]] for t in ts], axis=0)
        return acc + jnp.dot(wcat, scat, preferred_element_type=jnp.float32)

    acc = lax.fori_loop(0, groups, forward, jnp.zeros((rows, width), jnp.float32))
    deg = deg_ref[0]
    aggregate = (acc / deg).astype(jnp.bfloat16)
    own = hist_ref[0]
    logits = jnp.dot(aggregate, nw_ref[...], preferred_element_type=jnp.float32) + jnp.dot(
        own, sw_ref[...], preferred_element_type=jnp.float32
    )
    col = lax.broadcasted_iota(jnp.int32, (rows, padded), 1)
    logits = jnp.where(col < classes, logits, -1e30)
    top = jnp.max(logits, axis=-1, keepdims=True)
    expd = jnp.exp(logits - top)
    predicted = expd / jnp.sum(expd, axis=-1, keepdims=True)
    onehot = (col == lab_ref[0]).astype(jnp.float32)
    residual = predicted - onehot
    delta = residual.astype(jnp.bfloat16)
    tn = (((0,), (0,)), ((), ()))
    grads_ref[0] += lax.dot_general(aggregate, delta, tn, preferred_element_type=jnp.float32)
    grads_ref[1] += lax.dot_general(own, delta, tn, preferred_element_type=jnp.float32)
    selfterm_ref[0] = jnp.dot(delta, swt_ref[...], preferred_element_type=jnp.float32)
    scaled_t = (residual / deg).astype(jnp.bfloat16).T

    def backward(g, carry):
        for k in range(GROUP):
            t = g * GROUP + k
            s = src_ref[b, t]
            term_ref[s] += jnp.dot(scaled_t, tile(t), preferred_element_type=jnp.float32)
        return carry

    lax.fori_loop(0, groups, backward, 0)

    @pl.when(b == pl.num_programs(0) - 1)
    def _():
        out_ref[...] = term_ref[:, : out_ref.shape[1], :].astype(out_ref.dtype)


def _fused(tile_source, tile_live, tile_weight, sources, own_blocks, deg, lab, nw, sw, swt, classes):
    block_count, tile_slots, rows, _ = tile_weight.shape
    source_total, _, width = sources.shape
    padded = nw.shape[1]
    kept = -(-classes // 16) * 16
    grid_spec = pltpu.PrefetchScalarGridSpec(
        num_scalar_prefetch=2,
        grid=(block_count,),
        in_specs=[
            pl.BlockSpec((1, tile_slots, rows, rows), lambda b, *_: (b, 0, 0, 0)),
            pl.BlockSpec((source_total, rows, width), lambda b, *_: (0, 0, 0)),
            pl.BlockSpec((1, rows, width), lambda b, *_: (b, 0, 0)),
            pl.BlockSpec((1, rows, 1), lambda b, *_: (b, 0, 0)),
            pl.BlockSpec((1, rows, 1), lambda b, *_: (b, 0, 0)),
            pl.BlockSpec((width, padded), lambda b, *_: (0, 0)),
            pl.BlockSpec((width, padded), lambda b, *_: (0, 0)),
            pl.BlockSpec((padded, width), lambda b, *_: (0, 0)),
        ],
        out_specs=[
            pl.BlockSpec((source_total, kept, rows), lambda b, *_: (0, 0, 0)),
            pl.BlockSpec((2, width, padded), lambda b, *_: (0, 0, 0)),
            pl.BlockSpec((1, rows, width), lambda b, *_: (b, 0, 0)),
        ],
        scratch_shapes=[pltpu.VMEM((source_total, padded, rows), jnp.float32)],
    )
    return pl.pallas_call(
        functools.partial(_fused_kernel, classes=classes),
        grid_spec=grid_spec,
        out_shape=[
            jax.ShapeDtypeStruct((source_total, kept, rows), jnp.bfloat16),
            jax.ShapeDtypeStruct((2, width, padded), jnp.float32),
            jax.ShapeDtypeStruct((block_count, rows, width), jnp.float32),
        ],
        compiler_params=pltpu.CompilerParams(
            dimension_semantics=("arbitrary",), vmem_limit_bytes=60 * 1024 * 1024
        ),
    )(tile_source, tile_live, tile_weight, sources, own_blocks, deg, lab, nw, sw, swt)


def per_device(
    history,
    tile_weight,
    tile_source,
    tile_live,
    send_list,
    degree,
    labels,
    neigh_weight,
    self_weight,
):
    block_count = tile_weight.shape[0]
    block_rows = tile_weight.shape[2]
    width = history.shape[1]
    classes = neigh_weight.shape[1]
    dom_count = lax.axis_size("dom")
    sub_count = lax.axis_size("sub")
    devices_all = dom_count * sub_count
    nodes_all = history.shape[0] * devices_all
    padded = -(-classes // LANES) * LANES
    own_blocks = history.reshape(block_count, block_rows, width)
    partition = lax.all_gather(own_blocks, "sub", axis=0, tiled=True)
    part_blocks = partition.shape[0]
    own_ids = jnp.arange(block_count, dtype=jnp.int32)
    send_table = send_list[0][:, :, None] == own_ids[None, None, :]
    outgoing = jnp.einsum(
        "pks,sif->pkif",
        send_table.astype(jnp.bfloat16),
        own_blocks,
        preferred_element_type=jnp.float32,
    ).astype(jnp.bfloat16)
    boundary = lax.all_to_all(outgoing, "dom", split_axis=0, concat_axis=0, tiled=True)
    slot_count = boundary.shape[1]
    sources = jnp.concatenate(
        [partition, boundary.reshape(dom_count * slot_count, block_rows, width)], axis=0
    )
    degrees = degree.astype(jnp.float32).reshape(block_count, block_rows, 1)
    lab = labels.reshape(block_count, block_rows, 1)
    pad_cols = ((0, 0), (0, padded - classes))
    nw = jnp.pad(neigh_weight, pad_cols)
    sw = jnp.pad(self_weight, pad_cols)
    swt = jnp.pad(self_weight.T, ((0, padded - classes), (0, 0)))
    term, grads, selfterm = _fused(
        tile_source, tile_live, tile_weight, sources, own_blocks, degrees, lab, nw, sw, swt, classes
    )

    norm_factor = float(nodes_all) ** (-0.5)

    def split(x):
        hi = x.astype(jnp.bfloat16)
        return jnp.concatenate([hi, (x - hi.astype(jnp.float32)).astype(jnp.bfloat16)], axis=-1)

    def joined(x):
        half = x.shape[-1] // 2
        return x[..., :half].astype(jnp.float32) + x[..., half:].astype(jnp.float32)

    flat = grads[:, :, :classes].reshape(sub_count, -1)
    local = term[:part_blocks, :classes].reshape(sub_count, -1)
    local_size = local.shape[1]
    sent = jnp.concatenate([local, split(flat)], axis=1)
    got = lax.all_to_all(sent, "sub", 0, 0, tiled=True)
    local_grad = (
        got[:, :local_size].astype(jnp.float32).reshape(sub_count, block_count, classes, block_rows).sum(axis=0)
    )
    part_sum = joined(got[:, local_size:]).sum(axis=0).reshape(dom_count, -1)
    halo = term[part_blocks:, :classes].reshape(dom_count, -1)
    halo_size = halo.shape[1]
    sent = jnp.concatenate([halo, split(part_sum)], axis=1)
    got = lax.all_to_all(sent, "dom", 0, 0, tiled=True)
    arrived = got[:, :halo_size].astype(jnp.float32).reshape(dom_count, slot_count, classes, block_rows)
    mine = joined(got[:, halo_size:]).sum(axis=0, keepdims=True)
    spread = jnp.broadcast_to(mine, (devices_all, mine.shape[1]))
    totals = lax.all_to_all(spread, ("dom", "sub"), 0, 0, tiled=True)
    totals = totals.reshape(dom_count, sub_count, -1).transpose(1, 0, 2).reshape(2, width, classes)

    return_table = send_table.astype(jnp.float32)
    incoming = jnp.einsum("pks,pkci->sci", return_table, arrived, precision=lax.Precision.HIGHEST)
    backward_sum = local_grad + incoming
    neigh_float = neigh_weight.astype(jnp.float32)
    grad_history = jnp.einsum(
        "sci,fc->sif", backward_sum, neigh_float, precision=lax.Precision.HIGHEST
    ).reshape(-1, width) + selfterm.reshape(-1, width)
    return (grad_history, totals[0] * norm_factor, totals[1] * norm_factor)


def solution(mesh):
    placed = (
        P(("dom", "sub"), None),
        P(("dom", "sub"), None, None, None),
        P(("dom", "sub"), None),
        P(("dom", "sub")),
        P(("dom", "sub"), None, None),
        P(("dom", "sub")),
        P(("dom", "sub")),
        P(),
        P(),
    )
    return jax.shard_map(
        per_device,
        mesh=mesh,
        in_specs=placed,
        out_specs=(P(("dom", "sub"), None), P(), P()),
        check_vma=False,
    )
```

```python
import functools

import jax
import jax.numpy as jnp
from jax import lax
from jax.experimental import pallas as pl
from jax.experimental.pallas import tpu as pltpu
from jax.sharding import PartitionSpec as P

LANES = 128
GROUP = 8


def _fused_kernel(
    src_ref,
    live_ref,
    w_ref,
    sources_ref,
    hist_ref,
    deg_ref,
    lab_ref,
    nw_ref,
    sw_ref,
    swt_ref,
    out_ref,
    grads_ref,
    selfterm_ref,
    term_ref,
    *,
    classes,
):
    b = pl.program_id(0)
    rows = w_ref.shape[2]
    width = sources_ref.shape[2]
    padded = nw_ref.shape[1]

    @pl.when(b == 0)
    def _():
        term_ref[...] = jnp.zeros_like(term_ref)
        grads_ref[...] = jnp.zeros_like(grads_ref)

    live = live_ref[b]
    groups = (live + GROUP - 1) // GROUP

    def tile(t):
        return jnp.where(t < live, w_ref[0, t], jnp.zeros_like(w_ref[0, t]))

    def forward(g, acc):
        ts = [g * GROUP + k for k in range(GROUP)]
        wcat = jnp.concatenate([tile(t) for t in ts], axis=1)
        scat = jnp.concatenate([sources_ref[src_ref[b, t]] for t in ts], axis=0)
        return acc + jnp.dot(wcat, scat, preferred_element_type=jnp.float32)

    acc = lax.fori_loop(0, groups, forward, jnp.zeros((rows, width), jnp.float32))
    deg = deg_ref[0]
    aggregate = (acc / deg).astype(jnp.bfloat16)
    own = hist_ref[0]
    logits = jnp.dot(aggregate, nw_ref[...], preferred_element_type=jnp.float32) + jnp.dot(
        own, sw_ref[...], preferred_element_type=jnp.float32
    )
    col = lax.broadcasted_iota(jnp.int32, (rows, padded), 1)
    logits = jnp.where(col < classes, logits, -1e30)
    top = jnp.max(logits, axis=-1, keepdims=True)
    expd = jnp.exp(logits - top)
    predicted = expd / jnp.sum(expd, axis=-1, keepdims=True)
    onehot = (col == lab_ref[0]).astype(jnp.float32)
    residual = predicted - onehot
    delta = residual.astype(jnp.bfloat16)
    tn = (((0,), (0,)), ((), ()))
    grads_ref[0] += lax.dot_general(aggregate, delta, tn, preferred_element_type=jnp.float32)
    grads_ref[1] += lax.dot_general(own, delta, tn, preferred_element_type=jnp.float32)
    selfterm_ref[0] = jnp.dot(delta, swt_ref[...], preferred_element_type=jnp.float32)
    scaled_t = (residual / deg).astype(jnp.bfloat16).T

    def backward(g, carry):
        for k in range(GROUP):
            t = g * GROUP + k
            s = src_ref[b, t]
            term_ref[s] += jnp.dot(scaled_t, tile(t), preferred_element_type=jnp.float32)
        return carry

    lax.fori_loop(0, groups, backward, 0)

    @pl.when(b == pl.num_programs(0) - 1)
    def _():
        out_ref[...] = term_ref[:, : out_ref.shape[1], :].astype(out_ref.dtype)


def _fused(tile_source, tile_live, tile_weight, sources, own_blocks, deg, lab, nw, sw, swt, classes):
    block_count, tile_slots, rows, _ = tile_weight.shape
    source_total, _, width = sources.shape
    padded = nw.shape[1]
    kept = -(-classes // 16) * 16
    grid_spec = pltpu.PrefetchScalarGridSpec(
        num_scalar_prefetch=2,
        grid=(block_count,),
        in_specs=[
            pl.BlockSpec((1, tile_slots, rows, rows), lambda b, *_: (b, 0, 0, 0)),
            pl.BlockSpec((source_total, rows, width), lambda b, *_: (0, 0, 0)),
            pl.BlockSpec((1, rows, width), lambda b, *_: (b, 0, 0)),
            pl.BlockSpec((1, rows, 1), lambda b, *_: (b, 0, 0)),
            pl.BlockSpec((1, rows, 1), lambda b, *_: (b, 0, 0)),
            pl.BlockSpec((width, padded), lambda b, *_: (0, 0)),
            pl.BlockSpec((width, padded), lambda b, *_: (0, 0)),
            pl.BlockSpec((padded, width), lambda b, *_: (0, 0)),
        ],
        out_specs=[
            pl.BlockSpec((source_total, kept, rows), lambda b, *_: (0, 0, 0)),
            pl.BlockSpec((2, width, padded), lambda b, *_: (0, 0, 0)),
            pl.BlockSpec((1, rows, width), lambda b, *_: (b, 0, 0)),
        ],
        scratch_shapes=[pltpu.VMEM((source_total, padded, rows), jnp.float32)],
    )
    return pl.pallas_call(
        functools.partial(_fused_kernel, classes=classes),
        grid_spec=grid_spec,
        out_shape=[
            jax.ShapeDtypeStruct((source_total, kept, rows), jnp.bfloat16),
            jax.ShapeDtypeStruct((2, width, padded), jnp.float32),
            jax.ShapeDtypeStruct((block_count, rows, width), jnp.float32),
        ],
        compiler_params=pltpu.CompilerParams(
            dimension_semantics=("arbitrary",), vmem_limit_bytes=60 * 1024 * 1024
        ),
    )(tile_source, tile_live, tile_weight, sources, own_blocks, deg, lab, nw, sw, swt)


def per_device(
    history,
    tile_weight,
    tile_source,
    tile_live,
    send_list,
    degree,
    labels,
    neigh_weight,
    self_weight,
):
    block_count = tile_weight.shape[0]
    block_rows = tile_weight.shape[2]
    width = history.shape[1]
    classes = neigh_weight.shape[1]
    dom_count = lax.axis_size("dom")
    sub_count = lax.axis_size("sub")
    devices_all = dom_count * sub_count
    nodes_all = history.shape[0] * devices_all
    padded = -(-classes // LANES) * LANES
    own_blocks = history.reshape(block_count, block_rows, width)
    partition = lax.all_gather(own_blocks, "sub", axis=0, tiled=True)
    part_blocks = partition.shape[0]
    own_ids = jnp.arange(block_count, dtype=jnp.int32)
    send_table = send_list[0][:, :, None] == own_ids[None, None, :]
    outgoing = jnp.einsum(
        "pks,sif->pkif",
        send_table.astype(jnp.bfloat16),
        own_blocks,
        preferred_element_type=jnp.float32,
    ).astype(jnp.bfloat16)
    boundary = lax.all_to_all(outgoing, "dom", split_axis=0, concat_axis=0, tiled=True)
    slot_count = boundary.shape[1]
    sources = jnp.concatenate(
        [partition, boundary.reshape(dom_count * slot_count, block_rows, width)], axis=0
    )
    degrees = degree.astype(jnp.float32).reshape(block_count, block_rows, 1)
    lab = labels.reshape(block_count, block_rows, 1)
    pad_cols = ((0, 0), (0, padded - classes))
    nw = jnp.pad(neigh_weight, pad_cols)
    sw = jnp.pad(self_weight, pad_cols)
    swt = jnp.pad(self_weight.T, ((0, padded - classes), (0, 0)))
    term, grads, selfterm = _fused(
        tile_source, tile_live, tile_weight, sources, own_blocks, degrees, lab, nw, sw, swt, classes
    )

    norm_factor = float(nodes_all) ** (-0.5)
    kept = term.shape[1]

    def split(x, size):
        hi = x.astype(jnp.bfloat16)
        pair = jnp.concatenate([hi, (x - hi.astype(jnp.float32)).astype(jnp.bfloat16)], axis=-1)
        return jnp.pad(pair, ((0, 0), (0, size - pair.shape[1])))

    def joined(x, half):
        return x[:, :half].astype(jnp.float32) + x[:, half : 2 * half].astype(jnp.float32)

    flat = grads[:, :, :classes].reshape(sub_count, -1)
    chunk = flat.shape[1]
    extra = split(flat, kept * block_rows).reshape(sub_count, 1, kept, block_rows)
    local = term[:part_blocks].reshape(sub_count, block_count, kept, block_rows)
    got = lax.all_to_all(jnp.concatenate([local, extra], axis=1), "sub", 0, 0, tiled=True)
    local_grad = got[:, :block_count].astype(jnp.float32).sum(axis=0)
    part_sum = joined(got[:, block_count].reshape(sub_count, -1), chunk).sum(axis=0)
    part_sum = part_sum.reshape(dom_count, -1)
    piece = part_sum.shape[1]
    extra_rows = -(-2 * piece // (16 * block_rows)) * 16
    extra = split(part_sum, extra_rows * block_rows).reshape(dom_count, extra_rows, block_rows)
    halo = term[part_blocks:].reshape(dom_count, slot_count * kept, block_rows)
    got = lax.all_to_all(jnp.concatenate([halo, extra], axis=1), "dom", 0, 0, tiled=True)
    arrived = got[:, : slot_count * kept].astype(jnp.float32)
    arrived = arrived.reshape(dom_count, slot_count, kept, block_rows)
    mine = joined(got[:, slot_count * kept :].reshape(dom_count, -1), piece).sum(axis=0, keepdims=True)
    spread = jnp.broadcast_to(mine, (devices_all, piece))
    totals = lax.all_to_all(spread, ("dom", "sub"), 0, 0, tiled=True)
    totals = totals.reshape(dom_count, sub_count, -1).transpose(1, 0, 2).reshape(2, width, classes)

    return_table = send_table.astype(jnp.float32)
    incoming = jnp.einsum("pks,pkci->sci", return_table, arrived, precision=lax.Precision.HIGHEST)
    backward_sum = (local_grad + incoming)[:, :classes]
    neigh_float = neigh_weight.astype(jnp.float32)
    grad_history = jnp.einsum(
        "sci,fc->sif", backward_sum, neigh_float, precision=lax.Precision.HIGHEST
    ).reshape(-1, width) + selfterm.reshape(-1, width)
    return (grad_history, totals[0] * norm_factor, totals[1] * norm_factor)


def solution(mesh):
    placed = (
        P(("dom", "sub"), None),
        P(("dom", "sub"), None, None, None),
        P(("dom", "sub"), None),
        P(("dom", "sub")),
        P(("dom", "sub"), None, None),
        P(("dom", "sub")),
        P(("dom", "sub")),
        P(),
        P(),
    )
    return jax.shard_map(
        per_device,
        mesh=mesh,
        in_specs=placed,
        out_specs=(P(("dom", "sub"), None), P(), P()),
        check_vma=False,
    )
```

```python
import functools

import jax
import jax.numpy as jnp
from jax import lax
from jax.experimental import pallas as pl
from jax.experimental.pallas import tpu as pltpu
from jax.sharding import PartitionSpec as P

LANES = 128
GROUP = 8


def _fused_kernel(
    src_ref,
    live_ref,
    w_ref,
    sources_ref,
    hist_ref,
    deg_ref,
    lab_ref,
    nw_ref,
    sw_ref,
    swt_ref,
    out_ref,
    grads_ref,
    selfterm_ref,
    term_ref,
    *,
    classes,
):
    b = pl.program_id(0)
    rows = w_ref.shape[2]
    width = sources_ref.shape[2]
    padded = nw_ref.shape[1]

    @pl.when(b == 0)
    def _():
        term_ref[...] = jnp.zeros_like(term_ref)
        grads_ref[...] = jnp.zeros_like(grads_ref)

    live = live_ref[b]
    groups = (live + GROUP - 1) // GROUP

    def tile(t):
        return jnp.where(t < live, w_ref[0, t], jnp.zeros_like(w_ref[0, t]))

    def forward(g, acc):
        ts = [g * GROUP + k for k in range(GROUP)]
        wcat = jnp.concatenate([tile(t) for t in ts], axis=1)
        scat = jnp.concatenate([sources_ref[src_ref[b, t]] for t in ts], axis=0)
        return acc + jnp.dot(wcat, scat, preferred_element_type=jnp.float32)

    acc = lax.fori_loop(0, groups, forward, jnp.zeros((rows, width), jnp.float32))
    deg = deg_ref[0]
    aggregate = (acc / deg).astype(jnp.bfloat16)
    own = hist_ref[0]
    logits = jnp.dot(aggregate, nw_ref[...], preferred_element_type=jnp.float32) + jnp.dot(
        own, sw_ref[...], preferred_element_type=jnp.float32
    )
    col = lax.broadcasted_iota(jnp.int32, (rows, padded), 1)
    logits = jnp.where(col < classes, logits, -1e30)
    top = jnp.max(logits, axis=-1, keepdims=True)
    expd = jnp.exp(logits - top)
    predicted = expd / jnp.sum(expd, axis=-1, keepdims=True)
    onehot = (col == lab_ref[0]).astype(jnp.float32)
    residual = predicted - onehot
    delta = residual.astype(jnp.bfloat16)
    tn = (((0,), (0,)), ((), ()))
    grads_ref[0] += lax.dot_general(aggregate, delta, tn, preferred_element_type=jnp.float32)
    grads_ref[1] += lax.dot_general(own, delta, tn, preferred_element_type=jnp.float32)
    selfterm_ref[0] = jnp.dot(delta, swt_ref[...], preferred_element_type=jnp.float32)
    scaled_t = (residual / deg).astype(jnp.bfloat16).T

    def backward(g, carry):
        for k in range(GROUP):
            t = g * GROUP + k
            s = src_ref[b, t]
            term_ref[s] += jnp.dot(scaled_t, tile(t), preferred_element_type=jnp.float32)
        return carry

    lax.fori_loop(0, groups, backward, 0)

    @pl.when(b == pl.num_programs(0) - 1)
    def _():
        out_ref[...] = term_ref[:, : out_ref.shape[1], :].astype(out_ref.dtype)


def _fused(tile_source, tile_live, tile_weight, sources, own_blocks, deg, lab, nw, sw, swt, classes):
    block_count, tile_slots, rows, _ = tile_weight.shape
    source_total, _, width = sources.shape
    padded = nw.shape[1]
    kept = -(-classes // 16) * 16
    grid_spec = pltpu.PrefetchScalarGridSpec(
        num_scalar_prefetch=2,
        grid=(block_count,),
        in_specs=[
            pl.BlockSpec((1, tile_slots, rows, rows), lambda b, *_: (b, 0, 0, 0)),
            pl.BlockSpec((source_total, rows, width), lambda b, *_: (0, 0, 0)),
            pl.BlockSpec((1, rows, width), lambda b, *_: (b, 0, 0)),
            pl.BlockSpec((1, rows, 1), lambda b, *_: (b, 0, 0)),
            pl.BlockSpec((1, rows, 1), lambda b, *_: (b, 0, 0)),
            pl.BlockSpec((width, padded), lambda b, *_: (0, 0)),
            pl.BlockSpec((width, padded), lambda b, *_: (0, 0)),
            pl.BlockSpec((padded, width), lambda b, *_: (0, 0)),
        ],
        out_specs=[
            pl.BlockSpec((source_total, kept, rows), lambda b, *_: (0, 0, 0)),
            pl.BlockSpec((2, width, padded), lambda b, *_: (0, 0, 0)),
            pl.BlockSpec((1, rows, width), lambda b, *_: (b, 0, 0)),
        ],
        scratch_shapes=[pltpu.VMEM((source_total, padded, rows), jnp.float32)],
    )
    return pl.pallas_call(
        functools.partial(_fused_kernel, classes=classes),
        grid_spec=grid_spec,
        out_shape=[
            jax.ShapeDtypeStruct((source_total, kept, rows), jnp.bfloat16),
            jax.ShapeDtypeStruct((2, width, padded), jnp.float32),
            jax.ShapeDtypeStruct((block_count, rows, width), jnp.float32),
        ],
        compiler_params=pltpu.CompilerParams(
            dimension_semantics=("arbitrary",), vmem_limit_bytes=60 * 1024 * 1024
        ),
    )(tile_source, tile_live, tile_weight, sources, own_blocks, deg, lab, nw, sw, swt)


def per_device(
    history,
    tile_weight,
    tile_source,
    tile_live,
    send_list,
    degree,
    labels,
    neigh_weight,
    self_weight,
):
    block_count = tile_weight.shape[0]
    block_rows = tile_weight.shape[2]
    width = history.shape[1]
    classes = neigh_weight.shape[1]
    dom_count = lax.axis_size("dom")
    sub_count = lax.axis_size("sub")
    devices_all = dom_count * sub_count
    nodes_all = history.shape[0] * devices_all
    padded = -(-classes // LANES) * LANES
    own_blocks = history.reshape(block_count, block_rows, width)
    partition = lax.all_gather(own_blocks, "sub", axis=0, tiled=True)
    part_blocks = partition.shape[0]
    own_ids = jnp.arange(block_count, dtype=jnp.int32)
    send_table = send_list[0][:, :, None] == own_ids[None, None, :]
    outgoing = jnp.einsum(
        "pks,sif->pkif",
        send_table.astype(jnp.bfloat16),
        own_blocks,
        preferred_element_type=jnp.float32,
    ).astype(jnp.bfloat16)
    boundary = lax.all_to_all(outgoing, "dom", split_axis=0, concat_axis=0, tiled=True)
    slot_count = boundary.shape[1]
    sources = jnp.concatenate(
        [partition, boundary.reshape(dom_count * slot_count, block_rows, width)], axis=0
    )
    degrees = degree.astype(jnp.float32).reshape(block_count, block_rows, 1)
    lab = labels.reshape(block_count, block_rows, 1)
    pad_cols = ((0, 0), (0, padded - classes))
    nw = jnp.pad(neigh_weight, pad_cols)
    sw = jnp.pad(self_weight, pad_cols)
    swt = jnp.pad(self_weight.T, ((0, padded - classes), (0, 0)))
    term, grads, selfterm = _fused(
        tile_source, tile_live, tile_weight, sources, own_blocks, degrees, lab, nw, sw, swt, classes
    )

    norm_factor = float(nodes_all) ** (-0.5)
    kept = term.shape[1]

    def split(x, size):
        hi = x.astype(jnp.bfloat16)
        pair = jnp.concatenate([hi, (x - hi.astype(jnp.float32)).astype(jnp.bfloat16)], axis=-1)
        return jnp.pad(pair, ((0, 0), (0, size - pair.shape[1])))

    def joined(x, half):
        return x[:, :half].astype(jnp.float32) + x[:, half : 2 * half].astype(jnp.float32)

    local_grad = lax.psum_scatter(
        term[:part_blocks], "sub", scatter_dimension=0, tiled=True
    ).astype(jnp.float32)
    flat = grads[:, :, :classes].reshape(sub_count, -1)
    part_sum = lax.all_to_all(flat, "sub", 0, 0, tiled=True).sum(axis=0)
    part_sum = part_sum.reshape(dom_count, -1)
    piece = part_sum.shape[1]
    extra_rows = -(-2 * piece // (16 * block_rows)) * 16
    extra = split(part_sum, extra_rows * block_rows).reshape(dom_count, extra_rows, block_rows)
    halo = term[part_blocks:].reshape(dom_count, slot_count * kept, block_rows)
    got = lax.all_to_all(jnp.concatenate([halo, extra], axis=1), "dom", 0, 0, tiled=True)
    arrived = got[:, : slot_count * kept].astype(jnp.float32)
    arrived = arrived.reshape(dom_count, slot_count, kept, block_rows)
    mine = joined(got[:, slot_count * kept :].reshape(dom_count, -1), piece).sum(axis=0, keepdims=True)
    spread = jnp.broadcast_to(mine, (devices_all, piece))
    totals = lax.all_to_all(spread, ("dom", "sub"), 0, 0, tiled=True)
    totals = totals.reshape(dom_count, sub_count, -1).transpose(1, 0, 2).reshape(2, width, classes)

    return_table = send_table.astype(jnp.float32)
    incoming = jnp.einsum("pks,pkci->sci", return_table, arrived, precision=lax.Precision.HIGHEST)
    backward_sum = (local_grad + incoming)[:, :classes]
    neigh_float = neigh_weight.astype(jnp.float32)
    grad_history = jnp.einsum(
        "sci,fc->sif", backward_sum, neigh_float, precision=lax.Precision.HIGHEST
    ).reshape(-1, width) + selfterm.reshape(-1, width)
    return (grad_history, totals[0] * norm_factor, totals[1] * norm_factor)


def solution(mesh):
    placed = (
        P(("dom", "sub"), None),
        P(("dom", "sub"), None, None, None),
        P(("dom", "sub"), None),
        P(("dom", "sub")),
        P(("dom", "sub"), None, None),
        P(("dom", "sub")),
        P(("dom", "sub")),
        P(),
        P(),
    )
    return jax.shard_map(
        per_device,
        mesh=mesh,
        in_specs=placed,
        out_specs=(P(("dom", "sub"), None), P(), P()),
        check_vma=False,
    )
```

```python
import functools

import jax
import jax.numpy as jnp
from jax import lax
from jax.experimental import pallas as pl
from jax.experimental.pallas import tpu as pltpu
from jax.sharding import PartitionSpec as P


LANES = 128
GROUP = 8


def _tile(w_ref, t, live):
    return jnp.where(t < live, w_ref[0, t], jnp.zeros_like(w_ref[0, t]))


def _forward_kernel(
    src_ref,
    live_ref,
    w_ref,
    sources_ref,
    hist_ref,
    deg_ref,
    lab_ref,
    nw_ref,
    sw_ref,
    swt_ref,
    grads_ref,
    selfterm_ref,
    scaled_ref,
    *,
    classes,
):
    b = pl.program_id(0)
    rows = w_ref.shape[2]
    width = sources_ref.shape[2]
    padded = nw_ref.shape[1]

    @pl.when(b == 0)
    def _():
        grads_ref[...] = jnp.zeros_like(grads_ref)

    live = live_ref[b]
    groups = (live + GROUP - 1) // GROUP

    def forward(g, acc):
        ts = [g * GROUP + k for k in range(GROUP)]
        wcat = jnp.concatenate([_tile(w_ref, t, live) for t in ts], axis=1)
        scat = jnp.concatenate([sources_ref[src_ref[b, t]] for t in ts], axis=0)
        return acc + jnp.dot(wcat, scat, preferred_element_type=jnp.float32)

    acc = lax.fori_loop(0, groups, forward, jnp.zeros((rows, width), jnp.float32))
    deg = deg_ref[0]
    aggregate = (acc / deg).astype(jnp.bfloat16)
    own = hist_ref[0]
    logits = jnp.dot(aggregate, nw_ref[...], preferred_element_type=jnp.float32) + jnp.dot(
        own, sw_ref[...], preferred_element_type=jnp.float32
    )
    col = lax.broadcasted_iota(jnp.int32, (rows, padded), 1)
    logits = jnp.where(col < classes, logits, -1e30)
    top = jnp.max(logits, axis=-1, keepdims=True)
    expd = jnp.exp(logits - top)
    predicted = expd / jnp.sum(expd, axis=-1, keepdims=True)
    onehot = (col == lab_ref[0]).astype(jnp.float32)
    residual = predicted - onehot
    delta = residual.astype(jnp.bfloat16)
    tn = (((0,), (0,)), ((), ()))
    grads_ref[0] += lax.dot_general(aggregate, delta, tn, preferred_element_type=jnp.float32)
    grads_ref[1] += lax.dot_general(own, delta, tn, preferred_element_type=jnp.float32)
    selfterm_ref[0] = jnp.dot(delta, swt_ref[...], preferred_element_type=jnp.float32)
    scaled_ref[0] = (residual / deg).astype(jnp.bfloat16).T


def _backward_kernel(src_ref, live_ref, w_ref, scaled_ref, out_ref, term_ref):
    b = pl.program_id(0)

    @pl.when(b == 0)
    def _():
        term_ref[...] = jnp.zeros_like(term_ref)

    live = live_ref[b]
    groups = (live + GROUP - 1) // GROUP
    scaled_t = scaled_ref[0]

    def backward(g, carry):
        for k in range(GROUP):
            t = g * GROUP + k
            s = src_ref[b, t]
            term_ref[s] += jnp.dot(scaled_t, _tile(w_ref, t, live), preferred_element_type=jnp.float32)
        return carry

    lax.fori_loop(0, groups, backward, 0)

    @pl.when(b == pl.num_programs(0) - 1)
    def _():
        out_ref[...] = term_ref[:, : out_ref.shape[1], :].astype(out_ref.dtype)


def _fused(tile_source, tile_live, tile_weight, sources, own_blocks, deg, lab, nw, sw, swt, classes):
    block_count, tile_slots, rows, _ = tile_weight.shape
    source_total, _, width = sources.shape
    padded = nw.shape[1]
    kept = -(-classes // 16) * 16
    params = pltpu.CompilerParams(dimension_semantics=("arbitrary",), vmem_limit_bytes=60 * 1024 * 1024)
    w_spec = pl.BlockSpec((1, tile_slots, rows, rows), lambda b, *_: (b, 0, 0, 0))
    scaled_spec = pl.BlockSpec((1, padded, rows), lambda b, *_: (b, 0, 0))
    grid_spec = pltpu.PrefetchScalarGridSpec(
        num_scalar_prefetch=2,
        grid=(block_count,),
        in_specs=[
            w_spec,
            pl.BlockSpec((source_total, rows, width), lambda b, *_: (0, 0, 0)),
            pl.BlockSpec((1, rows, width), lambda b, *_: (b, 0, 0)),
            pl.BlockSpec((1, rows, 1), lambda b, *_: (b, 0, 0)),
            pl.BlockSpec((1, rows, 1), lambda b, *_: (b, 0, 0)),
            pl.BlockSpec((width, padded), lambda b, *_: (0, 0)),
            pl.BlockSpec((width, padded), lambda b, *_: (0, 0)),
            pl.BlockSpec((padded, width), lambda b, *_: (0, 0)),
        ],
        out_specs=[
            pl.BlockSpec((2, width, padded), lambda b, *_: (0, 0, 0)),
            pl.BlockSpec((1, rows, width), lambda b, *_: (b, 0, 0)),
            scaled_spec,
        ],
    )
    grads, selfterm, scaled = pl.pallas_call(
        functools.partial(_forward_kernel, classes=classes),
        grid_spec=grid_spec,
        out_shape=[
            jax.ShapeDtypeStruct((2, width, padded), jnp.float32),
            jax.ShapeDtypeStruct((block_count, rows, width), jnp.float32),
            jax.ShapeDtypeStruct((block_count, padded, rows), jnp.bfloat16),
        ],
        compiler_params=params,
    )(tile_source, tile_live, tile_weight, sources, own_blocks, deg, lab, nw, sw, swt)
    grid_spec = pltpu.PrefetchScalarGridSpec(
        num_scalar_prefetch=2,
        grid=(block_count,),
        in_specs=[w_spec, scaled_spec],
        out_specs=[pl.BlockSpec((source_total, kept, rows), lambda b, *_: (0, 0, 0))],
        scratch_shapes=[pltpu.VMEM((source_total, padded, rows), jnp.float32)],
    )
    (term,) = pl.pallas_call(
        _backward_kernel,
        grid_spec=grid_spec,
        out_shape=[jax.ShapeDtypeStruct((source_total, kept, rows), jnp.bfloat16)],
        compiler_params=params,
    )(tile_source, tile_live, tile_weight, scaled)
    return term, grads, selfterm


def _per_device(
    history,
    tile_weight,
    tile_source,
    tile_live,
    send_list,
    degree,
    labels,
    neigh_weight,
    self_weight,
):
    block_count = tile_weight.shape[0]
    block_rows = tile_weight.shape[2]
    width = history.shape[1]
    classes = neigh_weight.shape[1]
    dom_count = lax.axis_size("dom")
    sub_count = lax.axis_size("sub")
    devices_all = dom_count * sub_count
    nodes_all = history.shape[0] * devices_all
    padded = -(-classes // LANES) * LANES
    own_blocks = history.reshape(block_count, block_rows, width)
    partition = lax.all_gather(own_blocks, "sub", axis=0, tiled=True)
    part_blocks = partition.shape[0]
    own_ids = jnp.arange(block_count, dtype=jnp.int32)
    send_table = send_list[0][:, :, None] == own_ids[None, None, :]
    outgoing = jnp.einsum(
        "pks,sif->pkif",
        send_table.astype(jnp.bfloat16),
        own_blocks,
        preferred_element_type=jnp.float32,
    ).astype(jnp.bfloat16)
    boundary = lax.all_to_all(outgoing, "dom", split_axis=0, concat_axis=0, tiled=True)
    slot_count = boundary.shape[1]
    sources = jnp.concatenate(
        [partition, boundary.reshape(dom_count * slot_count, block_rows, width)], axis=0
    )
    degrees = degree.astype(jnp.float32).reshape(block_count, block_rows, 1)
    lab = labels.reshape(block_count, block_rows, 1)
    pad_cols = ((0, 0), (0, padded - classes))
    nw = jnp.pad(neigh_weight, pad_cols)
    sw = jnp.pad(self_weight, pad_cols)
    swt = jnp.pad(self_weight.T, ((0, padded - classes), (0, 0)))
    term, grads, selfterm = _fused(
        tile_source, tile_live, tile_weight, sources, own_blocks, degrees, lab, nw, sw, swt, classes
    )

    norm_factor = float(nodes_all) ** (-0.5)
    kept = term.shape[1]

    def split(x, size):
        hi = x.astype(jnp.bfloat16)
        pair = jnp.concatenate([hi, (x - hi.astype(jnp.float32)).astype(jnp.bfloat16)], axis=-1)
        return jnp.pad(pair, ((0, 0), (0, size - pair.shape[1])))

    def joined(x, half):
        return x[:, :half].astype(jnp.float32) + x[:, half : 2 * half].astype(jnp.float32)

    local_grad = lax.psum_scatter(
        term[:part_blocks], "sub", scatter_dimension=0, tiled=True
    ).astype(jnp.float32)
    flat = grads[:, :, :classes].reshape(sub_count, -1)
    part_sum = lax.all_to_all(flat, "sub", 0, 0, tiled=True)
    part_sum = part_sum.sum(axis=0)
    part_sum = part_sum.reshape(dom_count, -1)
    piece = part_sum.shape[1]
    extra_rows = -(-2 * piece // (16 * block_rows)) * 16
    extra = split(part_sum, extra_rows * block_rows).reshape(dom_count, extra_rows, block_rows)
    halo = term[part_blocks:].reshape(dom_count, slot_count * kept, block_rows)
    got = lax.all_to_all(jnp.concatenate([halo, extra], axis=1), "dom", 0, 0, tiled=True)
    arrived = got[:, : slot_count * kept].astype(jnp.float32)
    arrived = arrived.reshape(dom_count, slot_count, kept, block_rows)
    mine = joined(got[:, slot_count * kept :].reshape(dom_count, -1), piece).sum(axis=0, keepdims=True)
    spread = jnp.broadcast_to(mine, (devices_all, piece))
    totals = lax.all_to_all(spread, ("dom", "sub"), 0, 0, tiled=True)
    totals = totals.reshape(dom_count, sub_count, -1).transpose(1, 0, 2).reshape(2, width, classes)

    return_table = send_table.astype(jnp.float32)
    incoming = jnp.einsum("pks,pkci->sci", return_table, arrived, precision=lax.Precision.HIGHEST)
    backward_sum = (local_grad + incoming)[:, :classes]
    neigh_float = neigh_weight.astype(jnp.float32)
    grad_history = jnp.einsum(
        "sci,fc->sif", backward_sum, neigh_float, precision=lax.Precision.HIGHEST
    ).reshape(-1, width) + selfterm.reshape(-1, width)
    return (grad_history, totals[0] * norm_factor, totals[1] * norm_factor)


def solution(mesh):
    placed = (
        P(("dom", "sub"), None),
        P(("dom", "sub"), None, None, None),
        P(("dom", "sub"), None),
        P(("dom", "sub")),
        P(("dom", "sub"), None, None),
        P(("dom", "sub")),
        P(("dom", "sub")),
        P(),
        P(),
    )
    return jax.shard_map(
        _per_device,
        mesh=mesh,
        in_specs=placed,
        out_specs=(P(("dom", "sub"), None), P(), P()),
        check_vma=False,
    )
```

```python
import functools

import jax
import jax.numpy as jnp
from jax import lax
from jax.experimental import pallas as pl
from jax.experimental.pallas import tpu as pltpu
from jax.sharding import PartitionSpec as P


LANES = 128
GROUP = 8


def _tile(w_ref, t, live):
    return jnp.where(t < live, w_ref[0, t], jnp.zeros_like(w_ref[0, t]))


def _forward_kernel(
    src_ref,
    live_ref,
    w_ref,
    part_ref,
    bnd_ref,
    hist_ref,
    deg_ref,
    lab_ref,
    nw_ref,
    sw_ref,
    swt_ref,
    grads_ref,
    selfterm_ref,
    scaled_ref,
    *,
    classes,
):
    b = pl.program_id(0)
    rows = w_ref.shape[2]
    width = part_ref.shape[2]
    padded = nw_ref.shape[1]
    part_total = part_ref.shape[0]

    @pl.when(b == 0)
    def _():
        grads_ref[...] = jnp.zeros_like(grads_ref)

    def source(s):
        inside = part_ref[jnp.minimum(s, part_total - 1)]
        outside = bnd_ref[jnp.maximum(s - part_total, 0)]
        return jnp.where(s < part_total, inside, outside)

    live = live_ref[b]
    groups = (live + GROUP - 1) // GROUP

    def forward(g, acc):
        ts = [g * GROUP + k for k in range(GROUP)]
        wcat = jnp.concatenate([_tile(w_ref, t, live) for t in ts], axis=1)
        scat = jnp.concatenate([source(src_ref[b, t]) for t in ts], axis=0)
        return acc + jnp.dot(wcat, scat, preferred_element_type=jnp.float32)

    acc = lax.fori_loop(0, groups, forward, jnp.zeros((rows, width), jnp.float32))
    deg = deg_ref[0]
    aggregate = (acc / deg).astype(jnp.bfloat16)
    own = hist_ref[0]
    logits = jnp.dot(aggregate, nw_ref[...], preferred_element_type=jnp.float32) + jnp.dot(
        own, sw_ref[...], preferred_element_type=jnp.float32
    )
    col = lax.broadcasted_iota(jnp.int32, (rows, padded), 1)
    logits = jnp.where(col < classes, logits, -1e30)
    top = jnp.max(logits, axis=-1, keepdims=True)
    expd = jnp.exp(logits - top)
    predicted = expd / jnp.sum(expd, axis=-1, keepdims=True)
    onehot = (col == lab_ref[0]).astype(jnp.float32)
    residual = predicted - onehot
    delta = residual.astype(jnp.bfloat16)
    tn = (((0,), (0,)), ((), ()))
    grads_ref[0] += lax.dot_general(aggregate, delta, tn, preferred_element_type=jnp.float32)
    grads_ref[1] += lax.dot_general(own, delta, tn, preferred_element_type=jnp.float32)
    selfterm_ref[0] = jnp.dot(delta, swt_ref[...], preferred_element_type=jnp.float32)
    scaled_ref[0] = (residual / deg).astype(jnp.bfloat16).T


def _backward_kernel(src_ref, live_ref, w_ref, scaled_ref, out_ref, term_ref):
    b = pl.program_id(0)

    @pl.when(b == 0)
    def _():
        term_ref[...] = jnp.zeros_like(term_ref)

    live = live_ref[b]
    groups = (live + GROUP - 1) // GROUP
    scaled_t = scaled_ref[0]

    def backward(g, carry):
        for k in range(GROUP):
            t = g * GROUP + k
            s = src_ref[b, t]
            term_ref[s] += jnp.dot(scaled_t, _tile(w_ref, t, live), preferred_element_type=jnp.float32)
        return carry

    lax.fori_loop(0, groups, backward, 0)

    @pl.when(b == pl.num_programs(0) - 1)
    def _():
        out_ref[...] = term_ref[:, : out_ref.shape[1], :].astype(out_ref.dtype)


def _fused(tile_source, tile_live, tile_weight, partition, boundary, own_blocks, deg, lab, nw, sw, swt, classes):
    block_count, tile_slots, rows, _ = tile_weight.shape
    part_total, _, width = partition.shape
    source_total = part_total + boundary.shape[0]
    padded = nw.shape[1]
    kept = -(-classes // 16) * 16
    params = pltpu.CompilerParams(dimension_semantics=("arbitrary",), vmem_limit_bytes=60 * 1024 * 1024)
    w_spec = pl.BlockSpec((1, tile_slots, rows, rows), lambda b, *_: (b, 0, 0, 0))
    scaled_spec = pl.BlockSpec((1, padded, rows), lambda b, *_: (b, 0, 0))
    grid_spec = pltpu.PrefetchScalarGridSpec(
        num_scalar_prefetch=2,
        grid=(block_count,),
        in_specs=[
            w_spec,
            pl.BlockSpec(partition.shape, lambda b, *_: (0, 0, 0)),
            pl.BlockSpec(boundary.shape, lambda b, *_: (0, 0, 0)),
            pl.BlockSpec((1, rows, width), lambda b, *_: (b, 0, 0)),
            pl.BlockSpec((1, rows, 1), lambda b, *_: (b, 0, 0)),
            pl.BlockSpec((1, rows, 1), lambda b, *_: (b, 0, 0)),
            pl.BlockSpec((width, padded), lambda b, *_: (0, 0)),
            pl.BlockSpec((width, padded), lambda b, *_: (0, 0)),
            pl.BlockSpec((padded, width), lambda b, *_: (0, 0)),
        ],
        out_specs=[
            pl.BlockSpec((2, width, padded), lambda b, *_: (0, 0, 0)),
            pl.BlockSpec((1, rows, width), lambda b, *_: (b, 0, 0)),
            scaled_spec,
        ],
    )
    grads, selfterm, scaled = pl.pallas_call(
        functools.partial(_forward_kernel, classes=classes),
        grid_spec=grid_spec,
        out_shape=[
            jax.ShapeDtypeStruct((2, width, padded), jnp.float32),
            jax.ShapeDtypeStruct((block_count, rows, width), jnp.float32),
            jax.ShapeDtypeStruct((block_count, padded, rows), jnp.bfloat16),
        ],
        compiler_params=params,
    )(tile_source, tile_live, tile_weight, partition, boundary, own_blocks, deg, lab, nw, sw, swt)
    grid_spec = pltpu.PrefetchScalarGridSpec(
        num_scalar_prefetch=2,
        grid=(block_count,),
        in_specs=[w_spec, scaled_spec],
        out_specs=[pl.BlockSpec((source_total, kept, rows), lambda b, *_: (0, 0, 0))],
        scratch_shapes=[pltpu.VMEM((source_total, padded, rows), jnp.float32)],
    )
    (term,) = pl.pallas_call(
        _backward_kernel,
        grid_spec=grid_spec,
        out_shape=[jax.ShapeDtypeStruct((source_total, kept, rows), jnp.bfloat16)],
        compiler_params=params,
    )(tile_source, tile_live, tile_weight, scaled)
    return term, grads, selfterm


def _per_device(
    history,
    tile_weight,
    tile_source,
    tile_live,
    send_list,
    degree,
    labels,
    neigh_weight,
    self_weight,
):
    block_count = tile_weight.shape[0]
    block_rows = tile_weight.shape[2]
    width = history.shape[1]
    classes = neigh_weight.shape[1]
    dom_count = lax.axis_size("dom")
    sub_count = lax.axis_size("sub")
    devices_all = dom_count * sub_count
    nodes_all = history.shape[0] * devices_all
    padded = -(-classes // LANES) * LANES
    own_blocks = history.reshape(block_count, block_rows, width)
    partition = lax.all_gather(own_blocks, "sub", axis=0, tiled=True)
    part_blocks = partition.shape[0]
    own_ids = jnp.arange(block_count, dtype=jnp.int32)
    send_table = send_list[0][:, :, None] == own_ids[None, None, :]
    outgoing = jnp.take(own_blocks, send_list[0].reshape(-1), axis=0, mode="clip")
    outgoing = outgoing.reshape(send_list.shape[1:] + own_blocks.shape[1:])
    boundary = lax.all_to_all(outgoing, "dom", split_axis=0, concat_axis=0, tiled=True)
    slot_count = boundary.shape[1]
    boundary = boundary.reshape(dom_count * slot_count, block_rows, width)
    degrees = degree.astype(jnp.float32).reshape(block_count, block_rows, 1)
    lab = labels.reshape(block_count, block_rows, 1)
    pad_cols = ((0, 0), (0, padded - classes))
    nw = jnp.pad(neigh_weight, pad_cols)
    sw = jnp.pad(self_weight, pad_cols)
    swt = jnp.pad(self_weight.T, ((0, padded - classes), (0, 0)))
    term, grads, selfterm = _fused(
        tile_source, tile_live, tile_weight, partition, boundary, own_blocks, degrees, lab, nw, sw, swt, classes
    )

    norm_factor = float(nodes_all) ** (-0.5)
    kept = term.shape[1]

    def split(x, size):
        hi = x.astype(jnp.bfloat16)
        pair = jnp.concatenate([hi, (x - hi.astype(jnp.float32)).astype(jnp.bfloat16)], axis=-1)
        return jnp.pad(pair, ((0, 0), (0, size - pair.shape[1])))

    def joined(x, half):
        return x[:, :half].astype(jnp.float32) + x[:, half : 2 * half].astype(jnp.float32)

    local_grad = lax.psum_scatter(
        term[:part_blocks], "sub", scatter_dimension=0, tiled=True
    ).astype(jnp.float32)
    flat = grads[:, :, :classes].reshape(sub_count, -1)
    part_sum = lax.all_to_all(flat, "sub", 0, 0, tiled=True)
    part_sum = part_sum.sum(axis=0)
    part_sum = part_sum.reshape(dom_count, -1)
    piece = part_sum.shape[1]
    extra_rows = -(-2 * piece // (16 * block_rows)) * 16
    extra = split(part_sum, extra_rows * block_rows).reshape(dom_count, extra_rows, block_rows)
    halo = term[part_blocks:].reshape(dom_count, slot_count * kept, block_rows)
    got = lax.all_to_all(jnp.concatenate([halo, extra], axis=1), "dom", 0, 0, tiled=True)
    arrived = got[:, : slot_count * kept].astype(jnp.float32)
    arrived = arrived.reshape(dom_count, slot_count, kept, block_rows)
    mine = joined(got[:, slot_count * kept :].reshape(dom_count, -1), piece).sum(axis=0, keepdims=True)
    spread = jnp.broadcast_to(mine, (devices_all, piece))
    totals = lax.all_to_all(spread, ("dom", "sub"), 0, 0, tiled=True)
    totals = totals.reshape(dom_count, sub_count, -1).transpose(1, 0, 2).reshape(2, width, classes)

    return_table = send_table.astype(jnp.float32)
    incoming = jnp.einsum("pks,pkci->sci", return_table, arrived, precision=lax.Precision.HIGHEST)
    backward_sum = (local_grad + incoming)[:, :classes]
    neigh_float = neigh_weight.astype(jnp.float32)
    grad_history = jnp.einsum(
        "sci,fc->sif", backward_sum, neigh_float, precision=lax.Precision.HIGHEST
    ).reshape(-1, width) + selfterm.reshape(-1, width)
    return (grad_history, totals[0] * norm_factor, totals[1] * norm_factor)


def solution(mesh):
    placed = (
        P(("dom", "sub"), None),
        P(("dom", "sub"), None, None, None),
        P(("dom", "sub"), None),
        P(("dom", "sub")),
        P(("dom", "sub"), None, None),
        P(("dom", "sub")),
        P(("dom", "sub")),
        P(),
        P(),
    )
    return jax.shard_map(
        _per_device,
        mesh=mesh,
        in_specs=placed,
        out_specs=(P(("dom", "sub"), None), P(), P()),
        check_vma=False,
    )
```

```python
import functools

import jax
import jax.numpy as jnp
from jax import lax
from jax.experimental import pallas as pl
from jax.experimental.pallas import tpu as pltpu
from jax.sharding import PartitionSpec as P


LANES = 128
GROUP = 8


def _tile(w_ref, t, live):
    return jnp.where(t < live, w_ref[0, t], jnp.zeros_like(w_ref[0, t]))


def _forward_kernel(
    src_ref,
    live_ref,
    w_ref,
    part_ref,
    bnd_ref,
    hist_ref,
    deg_ref,
    lab_ref,
    nw_ref,
    sw_ref,
    swt_ref,
    grads_ref,
    selfterm_ref,
    scaled_ref,
    *,
    classes,
):
    b = pl.program_id(0)
    rows = w_ref.shape[2]
    width = part_ref.shape[2]
    padded = nw_ref.shape[1]
    part_total = part_ref.shape[0]

    @pl.when(b == 0)
    def _():
        grads_ref[...] = jnp.zeros_like(grads_ref)

    def source(s):
        inside = part_ref[jnp.minimum(s, part_total - 1)]
        outside = bnd_ref[jnp.maximum(s - part_total, 0)]
        return jnp.where(s < part_total, inside, outside)

    live = live_ref[b]
    groups = (live + GROUP - 1) // GROUP

    def forward(g, acc):
        ts = [g * GROUP + k for k in range(GROUP)]
        wcat = jnp.concatenate([_tile(w_ref, t, live) for t in ts], axis=1)
        scat = jnp.concatenate([source(src_ref[b, t]) for t in ts], axis=0)
        return acc + jnp.dot(wcat, scat, preferred_element_type=jnp.float32)

    acc = lax.fori_loop(0, groups, forward, jnp.zeros((rows, width), jnp.float32))
    deg = deg_ref[0]
    aggregate = (acc / deg).astype(jnp.bfloat16)
    own = hist_ref[0]
    logits = jnp.dot(aggregate, nw_ref[...], preferred_element_type=jnp.float32) + jnp.dot(
        own, sw_ref[...], preferred_element_type=jnp.float32
    )
    col = lax.broadcasted_iota(jnp.int32, (rows, padded), 1)
    logits = jnp.where(col < classes, logits, -1e30)
    top = jnp.max(logits, axis=-1, keepdims=True)
    expd = jnp.exp(logits - top)
    predicted = expd / jnp.sum(expd, axis=-1, keepdims=True)
    onehot = (col == lab_ref[0]).astype(jnp.float32)
    residual = predicted - onehot
    delta = residual.astype(jnp.bfloat16)
    tn = (((0,), (0,)), ((), ()))
    grads_ref[0] += lax.dot_general(aggregate, delta, tn, preferred_element_type=jnp.float32)
    grads_ref[1] += lax.dot_general(own, delta, tn, preferred_element_type=jnp.float32)
    selfterm_ref[0] = jnp.dot(delta, swt_ref[...], preferred_element_type=jnp.float32)
    scaled_ref[0] = (residual / deg).astype(jnp.bfloat16).T


def _backward_kernel(src_ref, live_ref, w_ref, scaled_ref, local_ref, halo_ref, term_ref, *, spare):
    b = pl.program_id(0)

    @pl.when(b == 0)
    def _():
        term_ref[...] = jnp.zeros_like(term_ref)

    live = live_ref[b]
    groups = (live + GROUP - 1) // GROUP
    scaled_t = scaled_ref[0]

    def backward(g, carry):
        for k in range(GROUP):
            t = g * GROUP + k
            s = src_ref[b, t]
            term_ref[s] += jnp.dot(scaled_t, _tile(w_ref, t, live), preferred_element_type=jnp.float32)
        return carry

    lax.fori_loop(0, groups, backward, 0)

    @pl.when(b == pl.num_programs(0) - 1)
    def _():
        part_total, kept, rows = local_ref.shape
        peers = halo_ref.shape[0]
        slots = (halo_ref.shape[1] - spare) // kept
        local_ref[...] = term_ref[:part_total, :kept, :].astype(local_ref.dtype)
        for p in range(peers):
            for k in range(slots):
                halo_ref[p, k * kept : (k + 1) * kept, :] = term_ref[
                    part_total + p * slots + k, :kept, :
                ].astype(halo_ref.dtype)
            halo_ref[p, slots * kept :, :] = jnp.zeros((spare, rows), halo_ref.dtype)


def _fused(
    tile_source, tile_live, tile_weight, partition, boundary, own_blocks, deg, lab, nw, sw, swt, classes, peers, spare
):
    block_count, tile_slots, rows, _ = tile_weight.shape
    part_total, _, width = partition.shape
    source_total = part_total + boundary.shape[0]
    padded = nw.shape[1]
    kept = -(-classes // 16) * 16
    params = pltpu.CompilerParams(dimension_semantics=("arbitrary",), vmem_limit_bytes=60 * 1024 * 1024)
    w_spec = pl.BlockSpec((1, tile_slots, rows, rows), lambda b, *_: (b, 0, 0, 0))
    scaled_spec = pl.BlockSpec((1, padded, rows), lambda b, *_: (b, 0, 0))
    grid_spec = pltpu.PrefetchScalarGridSpec(
        num_scalar_prefetch=2,
        grid=(block_count,),
        in_specs=[
            w_spec,
            pl.BlockSpec(partition.shape, lambda b, *_: (0, 0, 0)),
            pl.BlockSpec(boundary.shape, lambda b, *_: (0, 0, 0)),
            pl.BlockSpec((1, rows, width), lambda b, *_: (b, 0, 0)),
            pl.BlockSpec((1, rows, 1), lambda b, *_: (b, 0, 0)),
            pl.BlockSpec((1, rows, 1), lambda b, *_: (b, 0, 0)),
            pl.BlockSpec((width, padded), lambda b, *_: (0, 0)),
            pl.BlockSpec((width, padded), lambda b, *_: (0, 0)),
            pl.BlockSpec((padded, width), lambda b, *_: (0, 0)),
        ],
        out_specs=[
            pl.BlockSpec((2, width, padded), lambda b, *_: (0, 0, 0)),
            pl.BlockSpec((1, rows, width), lambda b, *_: (b, 0, 0)),
            scaled_spec,
        ],
    )
    grads, selfterm, scaled = pl.pallas_call(
        functools.partial(_forward_kernel, classes=classes),
        grid_spec=grid_spec,
        out_shape=[
            jax.ShapeDtypeStruct((2, width, padded), jnp.float32),
            jax.ShapeDtypeStruct((block_count, rows, width), jnp.float32),
            jax.ShapeDtypeStruct((block_count, padded, rows), jnp.bfloat16),
        ],
        compiler_params=params,
    )(tile_source, tile_live, tile_weight, partition, boundary, own_blocks, deg, lab, nw, sw, swt)
    halo_shape = (peers, (source_total - part_total) // peers * kept + spare, rows)
    grid_spec = pltpu.PrefetchScalarGridSpec(
        num_scalar_prefetch=2,
        grid=(block_count,),
        in_specs=[w_spec, scaled_spec],
        out_specs=[
            pl.BlockSpec((part_total, kept, rows), lambda b, *_: (0, 0, 0)),
            pl.BlockSpec(halo_shape, lambda b, *_: (0, 0, 0)),
        ],
        scratch_shapes=[pltpu.VMEM((source_total, padded, rows), jnp.float32)],
    )
    local, halo = pl.pallas_call(
        functools.partial(_backward_kernel, spare=spare),
        grid_spec=grid_spec,
        out_shape=[
            jax.ShapeDtypeStruct((part_total, kept, rows), jnp.bfloat16),
            jax.ShapeDtypeStruct(halo_shape, jnp.bfloat16),
        ],
        compiler_params=params,
    )(tile_source, tile_live, tile_weight, scaled)
    return local, halo, grads, selfterm


def _per_device(
    history,
    tile_weight,
    tile_source,
    tile_live,
    send_list,
    degree,
    labels,
    neigh_weight,
    self_weight,
):
    block_count = tile_weight.shape[0]
    block_rows = tile_weight.shape[2]
    width = history.shape[1]
    classes = neigh_weight.shape[1]
    dom_count = lax.axis_size("dom")
    sub_count = lax.axis_size("sub")
    devices_all = dom_count * sub_count
    nodes_all = history.shape[0] * devices_all
    padded = -(-classes // LANES) * LANES
    own_blocks = history.reshape(block_count, block_rows, width)
    partition = lax.all_gather(own_blocks, "sub", axis=0, tiled=True)
    own_ids = jnp.arange(block_count, dtype=jnp.int32)
    send_table = send_list[0][:, :, None] == own_ids[None, None, :]
    outgoing = jnp.take(own_blocks, send_list[0].reshape(-1), axis=0, mode="clip")
    outgoing = outgoing.reshape(send_list.shape[1:] + own_blocks.shape[1:])
    boundary = lax.all_to_all(outgoing, "dom", split_axis=0, concat_axis=0, tiled=True)
    slot_count = boundary.shape[1]
    boundary = boundary.reshape(dom_count * slot_count, block_rows, width)
    degrees = degree.astype(jnp.float32).reshape(block_count, block_rows, 1)
    lab = labels.reshape(block_count, block_rows, 1)
    pad_cols = ((0, 0), (0, padded - classes))
    nw = jnp.pad(neigh_weight, pad_cols)
    sw = jnp.pad(self_weight, pad_cols)
    swt = jnp.pad(self_weight.T, ((0, padded - classes), (0, 0)))
    kept = -(-classes // 16) * 16
    piece = 2 * width * classes // devices_all
    spare = -(-2 * piece // (16 * block_rows)) * 16
    local_term, halo_term, grads, selfterm = _fused(
        tile_source, tile_live, tile_weight, partition, boundary, own_blocks, degrees, lab, nw, sw, swt, classes,
        dom_count, spare,
    )

    norm_factor = float(nodes_all) ** (-0.5)

    def split(x, size):
        hi = x.astype(jnp.bfloat16)
        pair = jnp.concatenate([hi, (x - hi.astype(jnp.float32)).astype(jnp.bfloat16)], axis=-1)
        return jnp.pad(pair, ((0, 0), (0, size - pair.shape[1])))

    def joined(x, half):
        return x[:, :half].astype(jnp.float32) + x[:, half : 2 * half].astype(jnp.float32)

    local_grad = lax.psum_scatter(local_term, "sub", scatter_dimension=0, tiled=True).astype(jnp.float32)
    flat = grads[:, :, :classes].reshape(sub_count, -1)
    part_sum = lax.all_to_all(flat, "sub", 0, 0, tiled=True)
    part_sum = part_sum.sum(axis=0)
    part_sum = part_sum.reshape(dom_count, -1)
    extra = split(part_sum, spare * block_rows).reshape(dom_count, spare, block_rows)
    sent = lax.dynamic_update_slice(halo_term, extra, (0, slot_count * kept, 0))
    got = lax.all_to_all(sent, "dom", 0, 0, tiled=True)
    arrived = got[:, : slot_count * kept].astype(jnp.float32)
    arrived = arrived.reshape(dom_count, slot_count, kept, block_rows)
    mine = joined(got[:, slot_count * kept :].reshape(dom_count, -1), piece).sum(axis=0, keepdims=True)
    spread = jnp.broadcast_to(mine, (devices_all, piece))
    totals = lax.all_to_all(spread, ("dom", "sub"), 0, 0, tiled=True)
    totals = totals.reshape(dom_count, sub_count, -1).transpose(1, 0, 2).reshape(2, width, classes)

    return_table = send_table.astype(jnp.float32)
    incoming = jnp.einsum("pks,pkci->sci", return_table, arrived, precision=lax.Precision.HIGHEST)
    backward_sum = (local_grad + incoming)[:, :classes]
    neigh_float = neigh_weight.astype(jnp.float32)
    grad_history = jnp.einsum(
        "sci,fc->sif", backward_sum, neigh_float, precision=lax.Precision.HIGHEST
    ).reshape(-1, width) + selfterm.reshape(-1, width)
    return (grad_history, totals[0] * norm_factor, totals[1] * norm_factor)


def solution(mesh):
    placed = (
        P(("dom", "sub"), None),
        P(("dom", "sub"), None, None, None),
        P(("dom", "sub"), None),
        P(("dom", "sub")),
        P(("dom", "sub"), None, None),
        P(("dom", "sub")),
        P(("dom", "sub")),
        P(),
        P(),
    )
    return jax.shard_map(
        _per_device,
        mesh=mesh,
        in_specs=placed,
        out_specs=(P(("dom", "sub"), None), P(), P()),
        check_vma=False,
    )
```

```python
import functools

import jax
import jax.numpy as jnp
from jax import lax
from jax.experimental import pallas as pl
from jax.experimental.pallas import tpu as pltpu
from jax.sharding import PartitionSpec as P


LANES = 128
GROUP = 32
FORWARD_GROUP = 32


def _tile(w_ref, t, live):
    return jnp.where(t < live, w_ref[0, t], jnp.zeros_like(w_ref[0, t]))


def _forward_kernel(
    src_ref,
    live_ref,
    w_ref,
    part_ref,
    bnd_ref,
    hist_ref,
    deg_ref,
    lab_ref,
    nw_ref,
    sw_ref,
    swt_ref,
    grads_ref,
    selfterm_ref,
    scaled_ref,
    *,
    classes,
):
    b = pl.program_id(0)
    rows = w_ref.shape[2]
    width = part_ref.shape[2]
    padded = nw_ref.shape[1]
    part_total = part_ref.shape[0]

    @pl.when(b == 0)
    def _():
        grads_ref[...] = jnp.zeros_like(grads_ref)

    def source(s):
        inside = part_ref[jnp.minimum(s, part_total - 1)]
        outside = bnd_ref[jnp.maximum(s - part_total, 0)]
        return jnp.where(s < part_total, inside, outside)

    live = live_ref[b]
    groups = (live + FORWARD_GROUP - 1) // FORWARD_GROUP

    def forward(g, acc):
        ts = [g * FORWARD_GROUP + k for k in range(FORWARD_GROUP)]
        wcat = jnp.concatenate([_tile(w_ref, t, live) for t in ts], axis=1)
        scat = jnp.concatenate([source(src_ref[b, t]) for t in ts], axis=0)
        return acc + jnp.dot(wcat, scat, preferred_element_type=jnp.float32)

    acc = lax.fori_loop(0, groups, forward, jnp.zeros((rows, width), jnp.float32))
    deg = deg_ref[0]
    aggregate = (acc / deg).astype(jnp.bfloat16)
    own = hist_ref[0]
    logits = jnp.dot(aggregate, nw_ref[...], preferred_element_type=jnp.float32) + jnp.dot(
        own, sw_ref[...], preferred_element_type=jnp.float32
    )
    col = lax.broadcasted_iota(jnp.int32, (rows, padded), 1)
    logits = jnp.where(col < classes, logits, -1e30)
    top = jnp.max(logits, axis=-1, keepdims=True)
    expd = jnp.exp(logits - top)
    predicted = expd / jnp.sum(expd, axis=-1, keepdims=True)
    onehot = (col == lab_ref[0]).astype(jnp.float32)
    residual = predicted - onehot
    delta = residual.astype(jnp.bfloat16)
    tn = (((0,), (0,)), ((), ()))
    grads_ref[0] += lax.dot_general(aggregate, delta, tn, preferred_element_type=jnp.float32)
    grads_ref[1] += lax.dot_general(own, delta, tn, preferred_element_type=jnp.float32)
    selfterm_ref[0] = jnp.dot(delta, swt_ref[...], preferred_element_type=jnp.float32)
    scaled_ref[0] = (residual / deg).astype(jnp.bfloat16).T


def _backward_kernel(src_ref, live_ref, w_ref, scaled_ref, local_ref, halo_ref, term_ref, *, spare):
    b = pl.program_id(0)

    @pl.when(b == 0)
    def _():
        term_ref[...] = jnp.zeros_like(term_ref)

    live = live_ref[b]
    groups = (live + GROUP - 1) // GROUP
    scaled_t = scaled_ref[0]

    def backward(g, carry):
        for k in range(GROUP):
            t = g * GROUP + k
            s = src_ref[b, t]
            term_ref[s] += jnp.dot(scaled_t, _tile(w_ref, t, live), preferred_element_type=jnp.float32)
        return carry

    lax.fori_loop(0, groups, backward, 0)

    @pl.when(b == pl.num_programs(0) - 1)
    def _():
        part_total, kept, rows = local_ref.shape
        peers = halo_ref.shape[0]
        slots = (halo_ref.shape[1] - spare) // kept
        local_ref[...] = term_ref[:part_total, :kept, :].astype(local_ref.dtype)
        for p in range(peers):
            for k in range(slots):
                halo_ref[p, k * kept : (k + 1) * kept, :] = term_ref[
                    part_total + p * slots + k, :kept, :
                ].astype(halo_ref.dtype)
            halo_ref[p, slots * kept :, :] = jnp.zeros((spare, rows), halo_ref.dtype)


def _fused(
    tile_source, tile_live, tile_weight, partition, boundary, own_blocks, deg, lab, nw, sw, swt, classes, peers, spare
):
    block_count, tile_slots, rows, _ = tile_weight.shape
    part_total, _, width = partition.shape
    source_total = part_total + boundary.shape[0]
    padded = nw.shape[1]
    kept = -(-classes // 16) * 16
    params = pltpu.CompilerParams(dimension_semantics=("arbitrary",), vmem_limit_bytes=60 * 1024 * 1024)
    w_spec = pl.BlockSpec((1, tile_slots, rows, rows), lambda b, *_: (b, 0, 0, 0))
    scaled_spec = pl.BlockSpec((1, padded, rows), lambda b, *_: (b, 0, 0))
    grid_spec = pltpu.PrefetchScalarGridSpec(
        num_scalar_prefetch=2,
        grid=(block_count,),
        in_specs=[
            w_spec,
            pl.BlockSpec(partition.shape, lambda b, *_: (0, 0, 0)),
            pl.BlockSpec(boundary.shape, lambda b, *_: (0, 0, 0)),
            pl.BlockSpec((1, rows, width), lambda b, *_: (b, 0, 0)),
            pl.BlockSpec((1, rows, 1), lambda b, *_: (b, 0, 0)),
            pl.BlockSpec((1, rows, 1), lambda b, *_: (b, 0, 0)),
            pl.BlockSpec((width, padded), lambda b, *_: (0, 0)),
            pl.BlockSpec((width, padded), lambda b, *_: (0, 0)),
            pl.BlockSpec((padded, width), lambda b, *_: (0, 0)),
        ],
        out_specs=[
            pl.BlockSpec((2, width, padded), lambda b, *_: (0, 0, 0)),
            pl.BlockSpec((1, rows, width), lambda b, *_: (b, 0, 0)),
            scaled_spec,
        ],
    )
    grads, selfterm, scaled = pl.pallas_call(
        functools.partial(_forward_kernel, classes=classes),
        grid_spec=grid_spec,
        out_shape=[
            jax.ShapeDtypeStruct((2, width, padded), jnp.float32),
            jax.ShapeDtypeStruct((block_count, rows, width), jnp.float32),
            jax.ShapeDtypeStruct((block_count, padded, rows), jnp.bfloat16),
        ],
        compiler_params=params,
    )(tile_source, tile_live, tile_weight, partition, boundary, own_blocks, deg, lab, nw, sw, swt)
    halo_shape = (peers, (source_total - part_total) // peers * kept + spare, rows)
    grid_spec = pltpu.PrefetchScalarGridSpec(
        num_scalar_prefetch=2,
        grid=(block_count,),
        in_specs=[w_spec, scaled_spec],
        out_specs=[
            pl.BlockSpec((part_total, kept, rows), lambda b, *_: (0, 0, 0)),
            pl.BlockSpec(halo_shape, lambda b, *_: (0, 0, 0)),
        ],
        scratch_shapes=[pltpu.VMEM((source_total, padded, rows), jnp.float32)],
    )
    local, halo = pl.pallas_call(
        functools.partial(_backward_kernel, spare=spare),
        grid_spec=grid_spec,
        out_shape=[
            jax.ShapeDtypeStruct((part_total, kept, rows), jnp.bfloat16),
            jax.ShapeDtypeStruct(halo_shape, jnp.bfloat16),
        ],
        compiler_params=params,
    )(tile_source, tile_live, tile_weight, scaled)
    return local, halo, grads, selfterm


def _per_device(
    history,
    tile_weight,
    tile_source,
    tile_live,
    send_list,
    degree,
    labels,
    neigh_weight,
    self_weight,
):
    block_count = tile_weight.shape[0]
    block_rows = tile_weight.shape[2]
    width = history.shape[1]
    classes = neigh_weight.shape[1]
    dom_count = lax.axis_size("dom")
    sub_count = lax.axis_size("sub")
    devices_all = dom_count * sub_count
    nodes_all = history.shape[0] * devices_all
    padded = -(-classes // LANES) * LANES
    own_blocks = history.reshape(block_count, block_rows, width)
    partition = lax.all_gather(own_blocks, "sub", axis=0, tiled=True)
    own_ids = jnp.arange(block_count, dtype=jnp.int32)
    send_table = send_list[0][:, :, None] == own_ids[None, None, :]
    outgoing = jnp.take(own_blocks, send_list[0].reshape(-1), axis=0, mode="clip")
    outgoing = outgoing.reshape(send_list.shape[1:] + own_blocks.shape[1:])
    boundary = lax.all_to_all(outgoing, "dom", split_axis=0, concat_axis=0, tiled=True)
    slot_count = boundary.shape[1]
    boundary = boundary.reshape(dom_count * slot_count, block_rows, width)
    degrees = degree.astype(jnp.float32).reshape(block_count, block_rows, 1)
    lab = labels.reshape(block_count, block_rows, 1)
    pad_cols = ((0, 0), (0, padded - classes))
    nw = jnp.pad(neigh_weight, pad_cols)
    sw = jnp.pad(self_weight, pad_cols)
    swt = jnp.pad(self_weight.T, ((0, padded - classes), (0, 0)))
    kept = -(-classes // 16) * 16
    piece = 2 * width * classes // devices_all
    spare = -(-2 * piece // (16 * block_rows)) * 16
    local_term, halo_term, grads, selfterm = _fused(
        tile_source, tile_live, tile_weight, partition, boundary, own_blocks, degrees, lab, nw, sw, swt, classes,
        dom_count, spare,
    )

    norm_factor = float(nodes_all) ** (-0.5)

    def split(x, size):
        hi = x.astype(jnp.bfloat16)
        pair = jnp.concatenate([hi, (x - hi.astype(jnp.float32)).astype(jnp.bfloat16)], axis=-1)
        return jnp.pad(pair, ((0, 0), (0, size - pair.shape[1])))

    def joined(x, half):
        return x[:, :half].astype(jnp.float32) + x[:, half : 2 * half].astype(jnp.float32)

    local_grad = lax.psum_scatter(local_term, "sub", scatter_dimension=0, tiled=True).astype(jnp.float32)
    flat = grads[:, :, :classes].reshape(sub_count, -1)
    part_sum = lax.all_to_all(flat, "sub", 0, 0, tiled=True)
    part_sum = part_sum.sum(axis=0)
    part_sum = part_sum.reshape(dom_count, -1)
    extra = split(part_sum, spare * block_rows).reshape(dom_count, spare, block_rows)
    sent = lax.dynamic_update_slice(halo_term, extra, (0, slot_count * kept, 0))
    got = lax.all_to_all(sent, "dom", 0, 0, tiled=True)
    arrived = got[:, : slot_count * kept].astype(jnp.float32)
    arrived = arrived.reshape(dom_count, slot_count, kept, block_rows)
    mine = joined(got[:, slot_count * kept :].reshape(dom_count, -1), piece).sum(axis=0, keepdims=True)
    spread = jnp.broadcast_to(mine, (devices_all, piece))
    totals = lax.all_to_all(spread, ("dom", "sub"), 0, 0, tiled=True)
    totals = totals.reshape(dom_count, sub_count, -1).transpose(1, 0, 2).reshape(2, width, classes)

    return_table = send_table.astype(jnp.float32)
    incoming = jnp.einsum("pks,pkci->sci", return_table, arrived, precision=lax.Precision.HIGHEST)
    backward_sum = (local_grad + incoming)[:, :classes]
    neigh_float = neigh_weight.astype(jnp.float32)
    grad_history = jnp.einsum(
        "sci,fc->sif", backward_sum, neigh_float, precision=lax.Precision.HIGHEST
    ).reshape(-1, width) + selfterm.reshape(-1, width)
    return (grad_history, totals[0] * norm_factor, totals[1] * norm_factor)


def solution(mesh):
    placed = (
        P(("dom", "sub"), None),
        P(("dom", "sub"), None, None, None),
        P(("dom", "sub"), None),
        P(("dom", "sub")),
        P(("dom", "sub"), None, None),
        P(("dom", "sub")),
        P(("dom", "sub")),
        P(),
        P(),
    )
    return jax.shard_map(
        _per_device,
        mesh=mesh,
        in_specs=placed,
        out_specs=(P(("dom", "sub"), None), P(), P()),
        check_vma=False,
    )
```
